256 devices in a mesh: seq: 32 (over x, z), tensor: 8 (over y, core).
Axes of the slice: x: 4, y: 4, z: 8, core: 2. Of those that a mesh axis runs over, the one named last changes fastest.
Arguments:
- queries: bfloat16 [10240, 4096], P('seq', 'tensor'), may hold values from -8 to 8
- key_rows: bfloat16 [10240, 1024], P('seq', 'tensor'), may hold values from -8 to 8
- value_rows: bfloat16 [10240, 1024], P('seq', 'tensor'), may hold values from -6 to 6
- out_weight: bfloat16 [4096, 8192], P('tensor', 'seq'), may hold values from -0.09375 to 0.09375
- residual_in: bfloat16 [10240, 8192], P('seq'), may hold values from -0.1796875 to 0.1796875
- norm_gain: bfloat16 [8192], replicated, may hold values from 0.099609375 to 1.8984375
- prompt_lengths: int32 [18], replicated, may hold values from 1 to 5120, 10240 in all
Outputs:
- normed: bfloat16 [10240, 8192], P('seq')
- cache_keys: bfloat16 [22528, 1024], P('seq', 'tensor')
- cache_values: bfloat16 [22528, 1024], P('seq', 'tensor')
The draws below stay inside these ranges and needn't reach their ends.
Inputs may be any that keep to these rules, and one draw needn't show every extreme that they name: `prompt_lengths`: the 18 lengths sum to 10240, and the largest is 5120.
All inputs are finite; a program needn't handle non-finite values.
Results may differ from the reference program's by a relative error of at most 0.019.
Values may be sent and summed in bfloat16 or wider, within the bound.
No kernel may reach another device: no remote copies, remote signals or barrier semaphores. Data moves between devices by JAX's collectives and lax.ppermute only.
A program may use at most 192 MiB of HBM per device.

```python
import math
import jax
import jax.numpy as jnp
import numpy as np
from jax import lax

D = 8192
HD = 128
QPK = 4
SEQS = 18
PAGE = 128
TOK_DEV = 320
TOKENS = 10240
KVH = 8
QH = 32
SLOTS = 22528
N_SEQ = 32
N_TENSOR = 8


def draw_queries(key, part):
    width = QH * HD
    result = jnp.clip(jax.random.normal(jax.random.fold_in(key, 1), (TOKENS, width), jnp.float32), -6.0, 6.0)
    return result.astype(jnp.bfloat16)


def draw_key_rows(key, part):
    width = KVH * HD
    result = jnp.clip(jax.random.normal(jax.random.fold_in(key, 2), (TOKENS, width), jnp.float32), -6.0, 6.0)
    return result.astype(jnp.bfloat16)


def level_of(own_key, shape, split, smallest, largest):
    loudness, own = 1.0, jax.random.fold_in(own_key, 6)
    for dim, blocks in split:
        steps = jnp.exp(jax.random.uniform(jax.random.fold_in(own, dim), (blocks,), jnp.float32, smallest / len(split), largest / len(split)))
        loudness = loudness * jnp.repeat(steps, shape[dim] // blocks).reshape([-1 if axis == dim else 1 for axis in range(len(shape))])
    return loudness


def split_up(amount, total, most, slope):
    weights = [(1 << 20) // math.isqrt(rank ** slope) + 1 for rank in range(2, amount + 1)]
    surplus, counts = total - most - (amount - 1), [1] * (amount - 1)
    while surplus > 0:
        candidates = [i for i in range(amount - 1) if counts[i] < most]
        mass, budget = sum([weights[i] for i in candidates]), surplus
        for i in candidates:
            more = min(most - counts[i], max(1, budget * weights[i] // mass), surplus)
            counts[i] = counts[i] + more
            surplus = surplus - more
    return np.array([most] + counts)


def uneven_parts(own_key, count, total, limit, lean):
    if count == 2:
        one = jax.random.randint(own_key, (), max(1, total - limit), min(limit, total - 1) + 1)
        return jnp.stack([one, total - one])
    sizes = jnp.asarray(split_up(count, total, limit, lean), jnp.int32)
    twos = (count - 1) // 2
    donor, taker = sizes[1:1 + 2 * twos:2], sizes[2:2 + 2 * twos:2]
    margin = jnp.minimum(donor - 1, limit - taker)
    moved = jax.random.randint(jax.random.fold_in(own_key, 1), (twos,), 0, 1 << 20) % (margin + 1)
    sizes = sizes.at[1:1 + 2 * twos:2].set(donor - moved).at[2:2 + 2 * twos:2].set(taker + moved)
    return sizes[jax.random.permutation(jax.random.fold_in(own_key, 2), count)]


def gaussian(own_key, extent, scale, bound, cuts=(), held_as=jnp.bfloat16):
    array = jax.random.normal(own_key, extent, jnp.float32) * scale
    if len(cuts) > 0:
        array = level_of(own_key, extent, cuts, -0.22, 0.18) * array
    return jnp.clip(array, min=-bound, max=bound).astype(held_as)


def setup_inputs(seed: int = 0) -> dict:
    key_of = jax.random.split(jax.random.key(seed), 8)
    return {
        "queries": draw_queries(jax.random.fold_in(key_of[7], 71), 0),
        "key_rows": draw_key_rows(jax.random.fold_in(key_of[7], 71), 0),
        "value_rows": gaussian(key_of[2], (TOKENS, KVH * HD), 1.0, 6.0, ((0, 32), (1, 8))),
        "out_weight": gaussian(key_of[3], (QH * HD, D), (QH * HD) ** -0.5, 0.09375, ((0, 8), (1, 32))),
        "residual_in": gaussian(key_of[4], (TOKENS, D), 0.03, 0.1796875, ((0, 32),)),
        "norm_gain": jnp.clip(1.0 + 0.18 * jax.random.normal(key_of[5], (D,), jnp.float32), 0.099609375, 1.8984375).astype(jnp.bfloat16),
        "prompt_lengths": uneven_parts(key_of[6], SEQS, TOKENS, TOKENS // 2, 2).astype(jnp.int32),
    }


def position_of(stored, per_device, devices):
    half_block = per_device // 2
    device = stored // per_device
    offset = stored % per_device
    return jnp.where(offset < half_block, device * half_block + offset, (2 * devices - 1 - device) * half_block + offset - half_block).astype(jnp.int32)

def stored_row(position, per_device, devices):
    half_block = per_device // 2
    block_index = position // half_block
    device = jnp.where(block_index < devices, block_index, 2 * devices - 1 - block_index)
    offset = position % half_block + jnp.where(block_index < devices, 0, half_block)
    return (device * per_device + offset).astype(jnp.int32)

def segment_of(position, lengths):
    doc_ends = jnp.cumsum(lengths, dtype=jnp.int32)
    return lax.optimization_barrier(jnp.sum((position[:, None] >= doc_ends[None, :]).astype(jnp.int32), axis=1, dtype=jnp.int32))

def slot_source(slot_ids, lengths, page_size):
    padded = (lengths + page_size - 1) // page_size * page_size
    page_ends = jnp.cumsum(padded, dtype=jnp.int32)
    page_starts = page_ends - padded
    doc_ends = jnp.cumsum(lengths, dtype=jnp.int32)
    doc_starts = doc_ends - lengths
    prompt = lax.optimization_barrier(jnp.sum((slot_ids[:, None] >= page_ends[None, :]).astype(jnp.int32), axis=1, dtype=jnp.int32))
    clipped = jnp.minimum(prompt, lengths.shape[0] - 1)
    within = slot_ids - jnp.take(page_starts, clipped)
    is_live = (prompt < lengths.shape[0]) & (within < jnp.take(lengths, clipped))
    return ((jnp.take(doc_starts, clipped) + within).astype(jnp.int32), is_live)

def reference(queries, key_rows, value_rows, out_weight, residual_in, norm_gain, prompt_lengths):
    stored = jnp.arange(TOKENS, dtype=jnp.int32)
    position = position_of(stored, TOK_DEV, N_SEQ)
    segment = segment_of(position, prompt_lengths)
    score_scale = 1.0 / math.sqrt(HD)
    kv_heads = key_rows.shape[1] // HD
    key_float = key_rows.astype(jnp.float32).reshape(TOKENS, kv_heads, HD)
    value_float = value_rows.astype(jnp.float32).reshape(TOKENS, kv_heads, HD)
    query_blocks = queries.reshape(N_SEQ, TOK_DEV, kv_heads, QPK, HD)
    pos_blocks = position.reshape(N_SEQ, TOK_DEV)
    seg_blocks = segment.reshape(N_SEQ, TOK_DEV)

    def attend(block_inputs):
        query_block, query_pos, query_seg = block_inputs
        scores = jnp.einsum('qgjd,kgd->gjqk', query_block.astype(jnp.float32), key_float) * score_scale
        allowed = (position[None, :] <= query_pos[:, None]) & (segment[None, :] == query_seg[:, None])
        scores = jnp.where(allowed, scores, -1e+30)
        row_max = lax.optimization_barrier(jnp.max(scores, axis=-1, keepdims=True))
        weights = jnp.where(allowed, jnp.exp(scores - row_max), 0.0)
        totals = lax.optimization_barrier(jnp.sum(weights, axis=-1))
        rounded = lax.optimization_barrier(weights.astype(jnp.bfloat16)).astype(jnp.float32)
        summed = jnp.einsum('gjqk,kgd->qgjd', rounded, value_float)
        return (summed / jnp.transpose(totals, (2, 0, 1))[..., None]).astype(jnp.bfloat16)
    attended = lax.map(attend, (query_blocks, pos_blocks, seg_blocks)).reshape(TOKENS, -1)
    group_width = out_weight.shape[0] // N_TENSOR
    projected = jnp.zeros((TOKENS, out_weight.shape[1]), jnp.float32)
    for tensor_group in range(N_TENSOR):
        low = tensor_group * group_width
        partial_value = jnp.dot(attended[:, low:low + group_width], out_weight[low:low + group_width], preferred_element_type=jnp.float32)
        partial_value = lax.optimization_barrier(partial_value.astype(jnp.bfloat16)).astype(jnp.float32)
        projected = projected + partial_value
    hidden = residual_in.astype(jnp.float32) + projected
    mean_square = lax.optimization_barrier(jnp.mean(hidden * hidden, axis=-1, keepdims=True))
    normed = (hidden * lax.rsqrt(mean_square + 1e-05) * norm_gain.astype(jnp.float32)).astype(jnp.bfloat16)
    slot_ids = jnp.arange(SLOTS, dtype=jnp.int32)
    source, is_live = slot_source(slot_ids, prompt_lengths, PAGE)
    rows_at = jnp.clip(stored_row(source, TOK_DEV, N_SEQ), 0, TOKENS - 1).astype(jnp.int32)
    cache_keys = jnp.where(is_live[:, None], jnp.take(key_rows, rows_at, axis=0), jnp.zeros((), jnp.bfloat16))
    cache_values = jnp.where(is_live[:, None], jnp.take(value_rows, rows_at, axis=0), jnp.zeros((), jnp.bfloat16))
    return (normed, cache_keys, cache_values)
```

```python
import math

import jax
import jax.numpy as jnp
from jax import lax
from jax.sharding import PartitionSpec as P

HD = 128
PAGE = 128
SLOT_DEV = 704


def position_of(stored, per_device, devices):
    half_block = per_device // 2
    device = stored // per_device
    offset = stored % per_device
    return jnp.where(
        offset < half_block,
        device * half_block + offset,
        (2 * devices - 1 - device) * half_block + offset - half_block,
    )


def stored_row(position, per_device, devices):
    half_block = per_device // 2
    block_index = position // half_block
    device = jnp.where(block_index < devices, block_index, 2 * devices - 1 - block_index)
    offset = position % half_block + jnp.where(block_index < devices, 0, half_block)
    return device * per_device + offset


def segment_of(position, lengths):
    doc_ends = jnp.cumsum(lengths, dtype=jnp.int32)
    return jnp.sum(
        (position[:, None] >= doc_ends[None, :]).astype(jnp.int32), axis=1, dtype=jnp.int32
    )


def slot_source(slot_ids, lengths, page_size):
    padded = (lengths + page_size - 1) // page_size * page_size
    page_ends = jnp.cumsum(padded, dtype=jnp.int32)
    page_starts = page_ends - padded
    doc_ends = jnp.cumsum(lengths, dtype=jnp.int32)
    doc_starts = doc_ends - lengths
    before = (slot_ids[:, None] >= page_ends[None, :]).astype(jnp.int32)
    inside = (slot_ids[:, None] >= page_starts[None, :]).astype(jnp.int32) - before
    page_start = jnp.sum(before * padded[None, :], axis=1, dtype=jnp.int32)
    doc_start = jnp.sum(before * lengths[None, :], axis=1, dtype=jnp.int32)
    length = jnp.sum(inside * lengths[None, :], axis=1, dtype=jnp.int32)
    within = slot_ids - page_start
    is_live = within < length
    return (doc_start + within, is_live)


def body(queries, key_rows, value_rows, out_weight, residual_in, norm_gain, prompt_lengths):
    seq_count = lax.axis_size("seq")
    seq_index = lax.axis_index("seq")
    per_device = queries.shape[0]
    kv_local = key_rows.shape[1] // HD
    group_size = queries.shape[1] // (kv_local * HD)
    score_scale = 1.0 / math.sqrt(HD)
    local_rows = jnp.arange(per_device, dtype=jnp.int32) + seq_index * per_device
    my_position = position_of(local_rows, per_device, seq_count)
    my_segment = segment_of(my_position, prompt_lengths)
    grouped = queries.reshape(per_device, kv_local, group_size, HD)
    kv_width = key_rows.shape[1]
    kv_piece = lax.all_gather(
        jnp.concatenate([key_rows, value_rows], axis=1), "seq", axis=0, tiled=True
    )
    key_piece = kv_piece[:, :kv_width]
    value_piece = kv_piece[:, kv_width:]
    piece_rows = key_piece.shape[0]
    key_position = position_of(jnp.arange(piece_rows, dtype=jnp.int32), per_device, seq_count)
    key_segment = segment_of(key_position, prompt_lengths)
    allowed = (key_position[None, :] <= my_position[:, None]) & (
        key_segment[None, :] == my_segment[:, None]
    )
    top_old = jnp.full((kv_local, group_size, per_device), -1e30, jnp.float32)
    scores = (
        jnp.einsum(
            "qgjd,kgd->gjqk",
            grouped,
            key_piece.reshape(piece_rows, kv_local, HD),
            preferred_element_type=jnp.float32,
        )
        * score_scale
    )
    scores = jnp.where(allowed, scores, -1e30)
    top_new = jnp.maximum(top_old, jnp.max(scores, axis=-1))
    weights = jnp.where(allowed, jnp.exp(scores - top_new[..., None]), 0.0)
    total_new = jnp.sum(weights, axis=-1)
    accum_new = jnp.einsum(
        "gjqk,kgd->gjqd",
        weights.astype(jnp.bfloat16),
        value_piece.reshape(piece_rows, kv_local, HD),
        preferred_element_type=jnp.float32,
    )
    attended = jnp.transpose(accum_new / total_new[..., None], (2, 0, 1, 3))
    attended = attended.reshape(per_device, -1).astype(jnp.bfloat16)
    partial_value = jnp.dot(
        attended,
        lax.all_gather(out_weight, "seq", axis=1, tiled=True),
        preferred_element_type=jnp.float32,
    )
    projected = lax.psum(partial_value.astype(jnp.bfloat16), "tensor").astype(jnp.float32)
    hidden = residual_in.astype(jnp.float32) + projected
    mean_square = jnp.mean(hidden * hidden, axis=-1, keepdims=True)
    normed = (hidden * lax.rsqrt(mean_square + 1e-05) * norm_gain.astype(jnp.float32)).astype(
        jnp.bfloat16
    )
    slot_ids = seq_index * SLOT_DEV + jnp.arange(SLOT_DEV, dtype=jnp.int32)
    source, is_live = slot_source(slot_ids, prompt_lengths, PAGE)
    target = stored_row(source, per_device, seq_count)
    empty_cache = jnp.zeros((SLOT_DEV, kv_local * HD), jnp.bfloat16)
    found = is_live & (target >= 0) & (target < piece_rows)
    safe_index = jnp.clip(target, 0, piece_rows - 1)
    cache_keys = jnp.where(found[:, None], jnp.take(key_piece, safe_index, axis=0), empty_cache)
    cache_values = jnp.where(found[:, None], jnp.take(value_piece, safe_index, axis=0), empty_cache)
    return (normed, cache_keys, cache_values)


def solution(mesh):
    return jax.shard_map(
        body,
        mesh=mesh,
        in_specs=(
            P("seq", "tensor"),
            P("seq", "tensor"),
            P("seq", "tensor"),
            P("tensor", "seq"),
            P("seq", None),
            P(),
            P(),
        ),
        out_specs=(P("seq", None), P("seq", "tensor"), P("seq", "tensor")),
        check_vma=False,
    )
```

```python
import math

import jax
import jax.numpy as jnp
from jax import lax
from jax.sharding import PartitionSpec as P

HD = 128
PAGE = 128
SLOT_DEV = 704
MAX_PROMPT = 5120
SEQ_MINOR = 8


def position_of(stored, per_device, devices):
    half_block = per_device // 2
    device = stored // per_device
    offset = stored % per_device
    return jnp.where(
        offset < half_block,
        device * half_block + offset,
        (2 * devices - 1 - device) * half_block + offset - half_block,
    )


def stored_row(position, per_device, devices):
    half_block = per_device // 2
    block_index = position // half_block
    device = jnp.where(block_index < devices, block_index, 2 * devices - 1 - block_index)
    offset = position % half_block + jnp.where(block_index < devices, 0, half_block)
    return device * per_device + offset


def segment_of(position, lengths):
    doc_ends = jnp.cumsum(lengths, dtype=jnp.int32)
    return jnp.sum(
        (position[:, None] >= doc_ends[None, :]).astype(jnp.int32), axis=1, dtype=jnp.int32
    )


def slot_source(slot_ids, lengths, page_size):
    padded = (lengths + page_size - 1) // page_size * page_size
    page_ends = jnp.cumsum(padded, dtype=jnp.int32)
    page_starts = page_ends - padded
    doc_ends = jnp.cumsum(lengths, dtype=jnp.int32)
    doc_starts = doc_ends - lengths
    before = (slot_ids[:, None] >= page_ends[None, :]).astype(jnp.int32)
    inside = (slot_ids[:, None] >= page_starts[None, :]).astype(jnp.int32) - before
    page_start = jnp.sum(before * padded[None, :], axis=1, dtype=jnp.int32)
    doc_start = jnp.sum(before * lengths[None, :], axis=1, dtype=jnp.int32)
    length = jnp.sum(inside * lengths[None, :], axis=1, dtype=jnp.int32)
    within = slot_ids - page_start
    is_live = within < length
    return (doc_start + within, is_live)


def ring_offsets(n):
    forward = n // 2
    return [0] + [-r for r in range(1, forward + 1)] + [r for r in range(1, n - forward)]


def ring_collect(x, axis, n, stride, total):
    def shifted(shift):
        return [
            (i, (i // (n * stride)) * n * stride + ((i // stride) % n + shift) % n * stride + i % stride)
            for i in range(total)
        ]

    blocks = [x]
    forward = n // 2
    cur = x
    for _ in range(forward):
        cur = lax.ppermute(cur, axis, shifted(1))
        blocks.append(cur)
    cur = x
    for _ in range(n - 1 - forward):
        cur = lax.ppermute(cur, axis, shifted(-1))
        blocks.append(cur)
    return jnp.stack(blocks)


def ring_gather(x, axis, count, minor):
    outer = count // minor
    me = lax.axis_index(axis)
    stacked = ring_collect(x, axis, outer, minor, count)
    stacked = ring_collect(stacked, axis, minor, 1, count)
    stacked = stacked.reshape((count,) + x.shape)
    place_outer = [0] * outer
    for k, d in enumerate(ring_offsets(outer)):
        place_outer[d % outer] = k
    place_minor = [0] * minor
    for k, d in enumerate(ring_offsets(minor)):
        place_minor[d % minor] = k
    target = jnp.arange(count, dtype=jnp.int32)
    d_outer = (target // minor - me // minor) % outer
    d_minor = (target % minor - me % minor) % minor
    index = jnp.asarray(place_minor, jnp.int32)[d_minor] * outer + jnp.asarray(
        place_outer, jnp.int32
    )[d_outer]
    return jnp.take(stacked, index, axis=0)


def attend_block(query_block, block_index, kv_pos, lengths, half, kv_local, group_size, window):
    blocks = kv_pos.shape[0]
    start = jnp.clip(block_index - (window - 1), 0, blocks - window)
    kv_win = lax.dynamic_slice_in_dim(kv_pos, start, window, axis=0)
    kv_win = kv_win.reshape(window * half, -1)
    kv_width = kv_win.shape[1] // 2
    key_win = kv_win[:, :kv_width].reshape(window * half, kv_local, HD)
    value_win = kv_win[:, kv_width:].reshape(window * half, kv_local, HD)
    key_position = start * half + jnp.arange(window * half, dtype=jnp.int32)
    query_position = block_index * half + jnp.arange(half, dtype=jnp.int32)
    key_segment = segment_of(key_position, lengths)
    query_segment = segment_of(query_position, lengths)
    allowed = (key_position[None, :] <= query_position[:, None]) & (
        key_segment[None, :] == query_segment[:, None]
    )
    scores = (
        jnp.einsum("qgjd,kgd->gjqk", query_block, key_win, preferred_element_type=jnp.float32)
        * (1.0 / math.sqrt(HD))
    )
    scores = jnp.where(allowed, scores, -1e30)
    top = jnp.max(scores, axis=-1)
    weights = jnp.where(allowed, jnp.exp(scores - top[..., None]), 0.0)
    total = jnp.sum(weights, axis=-1)
    accum = jnp.einsum(
        "gjqk,kgd->gjqd",
        weights.astype(jnp.bfloat16),
        value_win,
        preferred_element_type=jnp.float32,
    )
    return jnp.transpose(accum / total[..., None], (2, 0, 1, 3))


def body(queries, key_rows, value_rows, out_weight, residual_in, norm_gain, prompt_lengths):
    seq_count = lax.axis_size("seq")
    seq_index = lax.axis_index("seq")
    per_device = queries.shape[0]
    half = per_device // 2
    kv_local = key_rows.shape[1] // HD
    group_size = queries.shape[1] // (kv_local * HD)
    kv_width = key_rows.shape[1]
    kv_piece = lax.all_gather(
        jnp.concatenate([key_rows, value_rows], axis=1), "seq", axis=0, tiled=True
    )
    weight_blocks = ring_gather(out_weight, "seq", seq_count, SEQ_MINOR)
    halves = kv_piece.reshape(seq_count, 2, half, 2 * kv_width)
    kv_pos = jnp.concatenate([halves[:, 0], halves[::-1, 1]], axis=0)
    window = min(2 * seq_count, (MAX_PROMPT - 1 + half - 1) // half + 1)
    grouped = queries.reshape(2, half, kv_local, group_size, HD)
    first = attend_block(
        grouped[0], seq_index, kv_pos, prompt_lengths, half, kv_local, group_size, window
    )
    second = attend_block(
        grouped[1], 2 * seq_count - 1 - seq_index, kv_pos, prompt_lengths, half, kv_local,
        group_size, window,
    )
    attended = jnp.concatenate([first, second], axis=0)
    attended = attended.reshape(per_device, -1).astype(jnp.bfloat16)
    partial_value = jnp.einsum(
        "qc,jcn->qjn", attended, weight_blocks, preferred_element_type=jnp.float32
    ).reshape(per_device, -1)
    projected = lax.psum(partial_value.astype(jnp.bfloat16), "tensor").astype(jnp.float32)
    hidden = residual_in.astype(jnp.float32) + projected
    mean_square = jnp.mean(hidden * hidden, axis=-1, keepdims=True)
    normed = (hidden * lax.rsqrt(mean_square + 1e-05) * norm_gain.astype(jnp.float32)).astype(
        jnp.bfloat16
    )
    slot_ids = seq_index * SLOT_DEV + jnp.arange(SLOT_DEV, dtype=jnp.int32)
    source, is_live = slot_source(slot_ids, prompt_lengths, PAGE)
    target = stored_row(source, per_device, seq_count)
    empty_cache = jnp.zeros((SLOT_DEV, kv_width), jnp.bfloat16)
    key_piece = kv_piece[:, :kv_width]
    value_piece = kv_piece[:, kv_width:]
    piece_rows = key_piece.shape[0]
    found = is_live & (target >= 0) & (target < piece_rows)
    safe_index = jnp.clip(target, 0, piece_rows - 1)
    cache_keys = jnp.where(found[:, None], jnp.take(key_piece, safe_index, axis=0), empty_cache)
    cache_values = jnp.where(found[:, None], jnp.take(value_piece, safe_index, axis=0), empty_cache)
    return (normed, cache_keys, cache_values)


def solution(mesh):
    return jax.shard_map(
        body,
        mesh=mesh,
        in_specs=(
            P("seq", "tensor"),
            P("seq", "tensor"),
            P("seq", "tensor"),
            P("tensor", "seq"),
            P("seq", None),
            P(),
            P(),
        ),
        out_specs=(P("seq", None), P("seq", "tensor"), P("seq", "tensor")),
        check_vma=False,
    )
```

```python
import math

import jax
import jax.numpy as jnp
from jax import lax
from jax.sharding import PartitionSpec as P

HD = 128
PAGE = 128
SLOT_DEV = 704
MAX_PROMPT = 5120


def position_of(stored, per_device, devices):
    half_block = per_device // 2
    device = stored // per_device
    offset = stored % per_device
    return jnp.where(
        offset < half_block,
        device * half_block + offset,
        (2 * devices - 1 - device) * half_block + offset - half_block,
    )


def stored_row(position, per_device, devices):
    half_block = per_device // 2
    block_index = position // half_block
    device = jnp.where(block_index < devices, block_index, 2 * devices - 1 - block_index)
    offset = position % half_block + jnp.where(block_index < devices, 0, half_block)
    return device * per_device + offset


def segment_of(position, lengths):
    doc_ends = jnp.cumsum(lengths, dtype=jnp.int32)
    return jnp.sum(
        (position[:, None] >= doc_ends[None, :]).astype(jnp.int32), axis=1, dtype=jnp.int32
    )


def slot_source(slot_ids, lengths, page_size):
    padded = (lengths + page_size - 1) // page_size * page_size
    page_ends = jnp.cumsum(padded, dtype=jnp.int32)
    page_starts = page_ends - padded
    doc_ends = jnp.cumsum(lengths, dtype=jnp.int32)
    doc_starts = doc_ends - lengths
    before = (slot_ids[:, None] >= page_ends[None, :]).astype(jnp.int32)
    inside = (slot_ids[:, None] >= page_starts[None, :]).astype(jnp.int32) - before
    page_start = jnp.sum(before * padded[None, :], axis=1, dtype=jnp.int32)
    doc_start = jnp.sum(before * lengths[None, :], axis=1, dtype=jnp.int32)
    length = jnp.sum(inside * lengths[None, :], axis=1, dtype=jnp.int32)
    within = slot_ids - page_start
    is_live = within < length
    return (doc_start + within, is_live)


def attend_block(query_block, block_index, kv_pos, lengths, half, kv_local, group_size, window):
    blocks = kv_pos.shape[0]
    start = jnp.clip(block_index - (window - 1), 0, blocks - window)
    kv_win = lax.dynamic_slice_in_dim(kv_pos, start, window, axis=0)
    kv_win = kv_win.reshape(window * half, -1)
    kv_width = kv_win.shape[1] // 2
    key_win = kv_win[:, :kv_width].reshape(window * half, kv_local, HD)
    value_win = kv_win[:, kv_width:].reshape(window * half, kv_local, HD)
    key_position = start * half + jnp.arange(window * half, dtype=jnp.int32)
    query_position = block_index * half + jnp.arange(half, dtype=jnp.int32)
    key_segment = segment_of(key_position, lengths)
    query_segment = segment_of(query_position, lengths)
    allowed = (key_position[None, :] <= query_position[:, None]) & (
        key_segment[None, :] == query_segment[:, None]
    )
    scores = (
        jnp.einsum("qgjd,kgd->gjqk", query_block, key_win, preferred_element_type=jnp.float32)
        * (1.0 / math.sqrt(HD))
    )
    scores = jnp.where(allowed, scores, -1e30)
    top = jnp.max(scores, axis=-1)
    weights = jnp.where(allowed, jnp.exp(scores - top[..., None]), 0.0)
    total = jnp.sum(weights, axis=-1)
    accum = jnp.einsum(
        "gjqk,kgd->gjqd",
        weights.astype(jnp.bfloat16),
        value_win,
        preferred_element_type=jnp.float32,
    )
    return jnp.transpose(accum / total[..., None], (2, 0, 1, 3))


def body(queries, key_rows, value_rows, out_weight, residual_in, norm_gain, prompt_lengths):
    seq_count = lax.axis_size("seq")
    seq_index = lax.axis_index("seq")
    per_device = queries.shape[0]
    half = per_device // 2
    kv_local = key_rows.shape[1] // HD
    group_size = queries.shape[1] // (kv_local * HD)
    kv_width = key_rows.shape[1]
    kv_rows = jnp.concatenate([key_rows, value_rows], axis=1)
    stacked = lax.all_gather(
        jnp.concatenate([kv_rows, out_weight], axis=0), "seq", axis=0, tiled=False
    )
    kv_piece = stacked[:, :per_device].reshape(seq_count * per_device, 2 * kv_width)
    weight_blocks = stacked[:, per_device:]
    halves = kv_piece.reshape(seq_count, 2, half, 2 * kv_width)
    kv_pos = jnp.concatenate([halves[:, 0], halves[::-1, 1]], axis=0)
    window = min(2 * seq_count, (MAX_PROMPT - 1 + half - 1) // half + 1)
    grouped = queries.reshape(2, half, kv_local, group_size, HD)
    first = attend_block(
        grouped[0], seq_index, kv_pos, prompt_lengths, half, kv_local, group_size, window
    )
    second = attend_block(
        grouped[1], 2 * seq_count - 1 - seq_index, kv_pos, prompt_lengths, half, kv_local,
        group_size, window,
    )
    attended = jnp.concatenate([first, second], axis=0)
    attended = attended.reshape(per_device, -1).astype(jnp.bfloat16)
    partial_value = jnp.einsum(
        "qc,jcn->qjn", attended, weight_blocks, preferred_element_type=jnp.float32
    ).reshape(per_device, -1)
    projected = lax.psum(partial_value.astype(jnp.bfloat16), "tensor").astype(jnp.float32)
    hidden = residual_in.astype(jnp.float32) + projected
    mean_square = jnp.mean(hidden * hidden, axis=-1, keepdims=True)
    normed = (hidden * lax.rsqrt(mean_square + 1e-05) * norm_gain.astype(jnp.float32)).astype(
        jnp.bfloat16
    )
    slot_ids = seq_index * SLOT_DEV + jnp.arange(SLOT_DEV, dtype=jnp.int32)
    source, is_live = slot_source(slot_ids, prompt_lengths, PAGE)
    target = stored_row(source, per_device, seq_count)
    empty_cache = jnp.zeros((SLOT_DEV, kv_width), jnp.bfloat16)
    key_piece = kv_piece[:, :kv_width]
    value_piece = kv_piece[:, kv_width:]
    piece_rows = key_piece.shape[0]
    found = is_live & (target >= 0) & (target < piece_rows)
    safe_index = jnp.clip(target, 0, piece_rows - 1)
    cache_keys = jnp.where(found[:, None], jnp.take(key_piece, safe_index, axis=0), empty_cache)
    cache_values = jnp.where(found[:, None], jnp.take(value_piece, safe_index, axis=0), empty_cache)
    return (normed, cache_keys, cache_values)


def solution(mesh):
    return jax.shard_map(
        body,
        mesh=mesh,
        in_specs=(
            P("seq", "tensor"),
            P("seq", "tensor"),
            P("seq", "tensor"),
            P("tensor", "seq"),
            P("seq", None),
            P(),
            P(),
        ),
        out_specs=(P("seq", None), P("seq", "tensor"), P("seq", "tensor")),
        check_vma=False,
    )
```

```python
import functools
import math

import jax
import jax.numpy as jnp
from jax import lax
from jax.experimental import pallas as pl
from jax.experimental.pallas import tpu as pltpu
from jax.sharding import PartitionSpec as P

HD = 128
PAGE = 128
SLOT_DEV = 704
MAX_PROMPT = 5120


def position_of(stored, per_device, devices):
    half_block = per_device // 2
    device = stored // per_device
    offset = stored % per_device
    return jnp.where(
        offset < half_block,
        device * half_block + offset,
        (2 * devices - 1 - device) * half_block + offset - half_block,
    )


def stored_row(position, per_device, devices):
    half_block = per_device // 2
    block_index = position // half_block
    device = jnp.where(block_index < devices, block_index, 2 * devices - 1 - block_index)
    offset = position % half_block + jnp.where(block_index < devices, 0, half_block)
    return device * per_device + offset


def segment_of(position, lengths):
    doc_ends = jnp.cumsum(lengths, dtype=jnp.int32)
    return jnp.sum(
        (position[:, None] >= doc_ends[None, :]).astype(jnp.int32), axis=1, dtype=jnp.int32
    )


def slot_source(slot_ids, lengths, page_size):
    padded = (lengths + page_size - 1) // page_size * page_size
    page_ends = jnp.cumsum(padded, dtype=jnp.int32)
    page_starts = page_ends - padded
    doc_ends = jnp.cumsum(lengths, dtype=jnp.int32)
    doc_starts = doc_ends - lengths
    before = (slot_ids[:, None] >= page_ends[None, :]).astype(jnp.int32)
    inside = (slot_ids[:, None] >= page_starts[None, :]).astype(jnp.int32) - before
    page_start = jnp.sum(before * padded[None, :], axis=1, dtype=jnp.int32)
    doc_start = jnp.sum(before * lengths[None, :], axis=1, dtype=jnp.int32)
    length = jnp.sum(inside * lengths[None, :], axis=1, dtype=jnp.int32)
    within = slot_ids - page_start
    is_live = within < length
    return (doc_start + within, is_live)


def attn_kernel(q_ref, kv_ref, qpos_ref, qseg_ref, kpos_ref, kseg_ref, o_ref, *, heads, scale):
    allowed = (kpos_ref[0] <= qpos_ref[0]) & (kseg_ref[0] == qseg_ref[0])
    key = kv_ref[0, :, :HD]
    value = kv_ref[0, :, HD:]
    for h in range(heads):
        query = q_ref[0, :, h * HD:(h + 1) * HD]
        scores = lax.dot_general(query, key, (((1,), (1,)), ((), ())),
                                 preferred_element_type=jnp.float32) * scale
        scores = jnp.where(allowed, scores, -1e30)
        top = jnp.max(scores, axis=1, keepdims=True)
        weights = jnp.where(allowed, jnp.exp(scores - top), 0.0)
        total = jnp.sum(weights, axis=1, keepdims=True)
        summed = jnp.dot(weights.astype(jnp.bfloat16), value, preferred_element_type=jnp.float32)
        o_ref[0, :, h * HD:(h + 1) * HD] = (summed / total).astype(o_ref.dtype)

def attend(q, kv, qpos, qseg, kpos, kseg):
    blocks, rows, width = q.shape
    window = kv.shape[1]
    heads = width // HD
    kern = functools.partial(attn_kernel, heads=heads, scale=1.0 / math.sqrt(HD))
    return pl.pallas_call(
        kern,
        grid=(blocks,),
        in_specs=[
            pl.BlockSpec((1, rows, width), lambda b: (b, 0, 0)),
            pl.BlockSpec((1, window, 2 * HD), lambda b: (b, 0, 0)),
            pl.BlockSpec((1, rows, 1), lambda b: (b, 0, 0)),
            pl.BlockSpec((1, rows, 1), lambda b: (b, 0, 0)),
            pl.BlockSpec((1, 1, window), lambda b: (b, 0, 0)),
            pl.BlockSpec((1, 1, window), lambda b: (b, 0, 0)),
        ],
        out_specs=pl.BlockSpec((1, rows, width), lambda b: (b, 0, 0)),
        out_shape=jax.ShapeDtypeStruct((blocks, rows, width), jnp.bfloat16),
        compiler_params=pltpu.CompilerParams(vmem_limit_bytes=48 * 1024 * 1024),
        cost_estimate=pl.CostEstimate(flops=4 * blocks * heads * rows * window * HD,
                                      transcendentals=blocks * heads * rows * window,
                                      bytes_accessed=blocks * (window * 2 * HD * 2 + 2 * rows * width * 2)),
    )(q, kv, qpos, qseg, kpos, kseg)

def body(queries, key_rows, value_rows, out_weight, residual_in, norm_gain, prompt_lengths):
    seq_count = lax.axis_size("seq")
    seq_index = lax.axis_index("seq")
    per_device = queries.shape[0]
    half = per_device // 2
    kv_width = key_rows.shape[1]
    kv_rows = jnp.concatenate([key_rows, value_rows], axis=1)
    stacked = lax.all_gather(
        jnp.concatenate([kv_rows, out_weight], axis=0), "seq", axis=1, tiled=True
    )
    weight_full = stacked[per_device:]
    kv_stored = jnp.transpose(
        stacked[:per_device].reshape(per_device, seq_count, 2 * kv_width), (1, 0, 2)
    )
    kv_piece = kv_stored.reshape(seq_count * per_device, 2 * kv_width)
    halves = kv_stored.reshape(seq_count, 2, half, 2 * kv_width)
    kv_pos = jnp.concatenate([halves[:, 0], halves[::-1, 1]], axis=0).reshape(
        seq_count * per_device, 2 * kv_width
    )
    window = min(seq_count * per_device, -(-(MAX_PROMPT - 1 + half) // 128) * 128)
    block_index = jnp.stack([seq_index, 2 * seq_count - 1 - seq_index])
    starts = jnp.clip(block_index * half + half - window, 0, seq_count * per_device - window)
    kv_win = jnp.stack(
        [lax.dynamic_slice_in_dim(kv_pos, starts[i], window, axis=0) for i in range(2)]
    )
    key_position = starts[:, None] + jnp.arange(window, dtype=jnp.int32)[None, :]
    query_position = block_index[:, None] * half + jnp.arange(half, dtype=jnp.int32)[None, :]
    key_segment = segment_of(key_position.reshape(-1), prompt_lengths).reshape(2, 1, window)
    query_segment = segment_of(query_position.reshape(-1), prompt_lengths).reshape(2, half, 1)
    attended = attend(
        queries.reshape(2, half, queries.shape[1]),
        kv_win,
        query_position[:, :, None],
        query_segment,
        key_position[:, None, :],
        key_segment,
    ).reshape(per_device, -1)
    partial_value = jnp.dot(attended, weight_full, preferred_element_type=jnp.float32)
    projected = lax.psum(partial_value.astype(jnp.bfloat16), "tensor").astype(jnp.float32)
    hidden = residual_in.astype(jnp.float32) + projected
    mean_square = jnp.mean(hidden * hidden, axis=-1, keepdims=True)
    normed = (hidden * lax.rsqrt(mean_square + 1e-05) * norm_gain.astype(jnp.float32)).astype(
        jnp.bfloat16
    )
    slot_ids = seq_index * SLOT_DEV + jnp.arange(SLOT_DEV, dtype=jnp.int32)
    source, is_live = slot_source(slot_ids, prompt_lengths, PAGE)
    target = stored_row(source, per_device, seq_count)
    empty_cache = jnp.zeros((SLOT_DEV, kv_width), jnp.bfloat16)
    key_piece = kv_piece[:, :kv_width]
    value_piece = kv_piece[:, kv_width:]
    piece_rows = key_piece.shape[0]
    found = is_live & (target >= 0) & (target < piece_rows)
    safe_index = jnp.clip(target, 0, piece_rows - 1)
    cache_keys = jnp.where(found[:, None], jnp.take(key_piece, safe_index, axis=0), empty_cache)
    cache_values = jnp.where(found[:, None], jnp.take(value_piece, safe_index, axis=0), empty_cache)
    return (normed, cache_keys, cache_values)


def solution(mesh):
    return jax.shard_map(
        body,
        mesh=mesh,
        in_specs=(
            P("seq", "tensor"),
            P("seq", "tensor"),
            P("seq", "tensor"),
            P("tensor", "seq"),
            P("seq", None),
            P(),
            P(),
        ),
        out_specs=(P("seq", None), P("seq", "tensor"), P("seq", "tensor")),
        check_vma=False,
    )
```

```python
import functools
import math

import jax
import jax.numpy as jnp
from jax import lax
from jax.experimental import pallas as pl
from jax.experimental.pallas import tpu as pltpu
from jax.sharding import PartitionSpec as P

HD = 128
PAGE = 128
SLOT_DEV = 704
MAX_PROMPT = 5120


def position_of(stored, per_device, devices):
    half_block = per_device // 2
    device = stored // per_device
    offset = stored % per_device
    return jnp.where(
        offset < half_block,
        device * half_block + offset,
        (2 * devices - 1 - device) * half_block + offset - half_block,
    )


def stored_row(position, per_device, devices):
    half_block = per_device // 2
    block_index = position // half_block
    device = jnp.where(block_index < devices, block_index, 2 * devices - 1 - block_index)
    offset = position % half_block + jnp.where(block_index < devices, 0, half_block)
    return device * per_device + offset


def segment_of(position, lengths):
    doc_ends = jnp.cumsum(lengths, dtype=jnp.int32)
    return jnp.sum(
        (position[:, None] >= doc_ends[None, :]).astype(jnp.int32), axis=1, dtype=jnp.int32
    )


def slot_source(slot_ids, lengths, page_size):
    padded = (lengths + page_size - 1) // page_size * page_size
    page_ends = jnp.cumsum(padded, dtype=jnp.int32)
    page_starts = page_ends - padded
    doc_ends = jnp.cumsum(lengths, dtype=jnp.int32)
    doc_starts = doc_ends - lengths
    before = (slot_ids[:, None] >= page_ends[None, :]).astype(jnp.int32)
    inside = (slot_ids[:, None] >= page_starts[None, :]).astype(jnp.int32) - before
    page_start = jnp.sum(before * padded[None, :], axis=1, dtype=jnp.int32)
    doc_start = jnp.sum(before * lengths[None, :], axis=1, dtype=jnp.int32)
    length = jnp.sum(inside * lengths[None, :], axis=1, dtype=jnp.int32)
    within = slot_ids - page_start
    is_live = within < length
    return (doc_start + within, is_live)


def attn_kernel(q_ref, kv_ref, qpos_ref, qseg_ref, kpos_ref, kseg_ref, o_ref, *, heads, scale):
    allowed = (kpos_ref[0] <= qpos_ref[0]) & (kseg_ref[0] == qseg_ref[0])
    key = kv_ref[0, :, :HD]
    value = kv_ref[0, :, HD:]
    for h in range(heads):
        query = q_ref[0, :, h * HD:(h + 1) * HD]
        scores = lax.dot_general(query, key, (((1,), (1,)), ((), ())),
                                 preferred_element_type=jnp.float32) * scale
        scores = jnp.where(allowed, scores, -1e30)
        top = jnp.max(scores, axis=1, keepdims=True)
        weights = jnp.where(allowed, jnp.exp(scores - top), 0.0)
        total = jnp.sum(weights, axis=1, keepdims=True)
        summed = jnp.dot(weights.astype(jnp.bfloat16), value, preferred_element_type=jnp.float32)
        o_ref[0, :, h * HD:(h + 1) * HD] = (summed / total).astype(o_ref.dtype)

def attend(q, kv, qpos, qseg, kpos, kseg):
    blocks, rows, width = q.shape
    window = kv.shape[1]
    heads = width // HD
    kern = functools.partial(attn_kernel, heads=heads, scale=1.0 / math.sqrt(HD))
    return pl.pallas_call(
        kern,
        grid=(blocks,),
        in_specs=[
            pl.BlockSpec((1, rows, width), lambda b: (b, 0, 0)),
            pl.BlockSpec((1, window, 2 * HD), lambda b: (b, 0, 0)),
            pl.BlockSpec((1, rows, 1), lambda b: (b, 0, 0)),
            pl.BlockSpec((1, rows, 1), lambda b: (b, 0, 0)),
            pl.BlockSpec((1, 1, window), lambda b: (b, 0, 0)),
            pl.BlockSpec((1, 1, window), lambda b: (b, 0, 0)),
        ],
        out_specs=pl.BlockSpec((1, rows, width), lambda b: (b, 0, 0)),
        out_shape=jax.ShapeDtypeStruct((blocks, rows, width), jnp.bfloat16),
        compiler_params=pltpu.CompilerParams(vmem_limit_bytes=48 * 1024 * 1024),
        cost_estimate=pl.CostEstimate(flops=4 * blocks * heads * rows * window * HD,
                                      transcendentals=blocks * heads * rows * window,
                                      bytes_accessed=blocks * (window * 2 * HD * 2 + 2 * rows * width * 2)),
    )(q, kv, qpos, qseg, kpos, kseg)

def norm_kernel(projected_ref, residual_ref, gain_ref, out_ref):
    hidden = residual_ref[...].astype(jnp.float32) + projected_ref[...].astype(jnp.float32)
    mean_square = jnp.mean(hidden * hidden, axis=-1, keepdims=True)
    out_ref[...] = (
        hidden * lax.rsqrt(mean_square + 1e-05) * gain_ref[...].astype(jnp.float32)
    ).astype(out_ref.dtype)


def residual_norm(projected, residual, gain, rows_per_step=40):
    rows, width = projected.shape
    steps = rows // rows_per_step
    return pl.pallas_call(
        norm_kernel,
        grid=(steps,),
        in_specs=[
            pl.BlockSpec((rows_per_step, width), lambda i: (i, 0)),
            pl.BlockSpec((rows_per_step, width), lambda i: (i, 0)),
            pl.BlockSpec((1, width), lambda i: (0, 0)),
        ],
        out_specs=pl.BlockSpec((rows_per_step, width), lambda i: (i, 0)),
        out_shape=jax.ShapeDtypeStruct((rows, width), jnp.bfloat16),
        cost_estimate=pl.CostEstimate(
            flops=5 * rows * width, transcendentals=rows, bytes_accessed=6 * rows * width
        ),
    )(projected, residual, gain.reshape(1, width))


def body(queries, key_rows, value_rows, out_weight, residual_in, norm_gain, prompt_lengths):
    seq_count = lax.axis_size("seq")
    seq_index = lax.axis_index("seq")
    per_device = queries.shape[0]
    half = per_device // 2
    kv_width = key_rows.shape[1]
    kv_rows = jnp.concatenate([key_rows, value_rows], axis=1)
    stacked = lax.all_gather(
        jnp.concatenate([kv_rows, out_weight], axis=0), "seq", axis=1, tiled=True
    )
    weight_full = stacked[per_device:]
    kv_stored = jnp.transpose(
        stacked[:per_device].reshape(per_device, seq_count, 2 * kv_width), (1, 0, 2)
    )
    kv_piece = kv_stored.reshape(seq_count * per_device, 2 * kv_width)
    halves = kv_stored.reshape(seq_count, 2, half, 2 * kv_width)
    kv_pos = jnp.concatenate([halves[:, 0], halves[::-1, 1]], axis=0).reshape(
        seq_count * per_device, 2 * kv_width
    )
    window = min(seq_count * per_device, -(-(MAX_PROMPT - 1 + half) // 128) * 128)
    block_index = jnp.stack([seq_index, 2 * seq_count - 1 - seq_index])
    starts = jnp.clip(block_index * half + half - window, 0, seq_count * per_device - window)
    kv_win = jnp.stack(
        [lax.dynamic_slice_in_dim(kv_pos, starts[i], window, axis=0) for i in range(2)]
    )
    key_position = starts[:, None] + jnp.arange(window, dtype=jnp.int32)[None, :]
    query_position = block_index[:, None] * half + jnp.arange(half, dtype=jnp.int32)[None, :]
    key_segment = segment_of(key_position.reshape(-1), prompt_lengths).reshape(2, 1, window)
    query_segment = segment_of(query_position.reshape(-1), prompt_lengths).reshape(2, half, 1)
    attended = attend(
        queries.reshape(2, half, queries.shape[1]),
        kv_win,
        query_position[:, :, None],
        query_segment,
        key_position[:, None, :],
        key_segment,
    ).reshape(per_device, -1)
    partial_value = jnp.dot(attended, weight_full, preferred_element_type=jnp.float32)
    projected = lax.psum(partial_value.astype(jnp.bfloat16), "tensor")
    normed = residual_norm(projected, residual_in, norm_gain)
    slot_ids = seq_index * SLOT_DEV + jnp.arange(SLOT_DEV, dtype=jnp.int32)
    source, is_live = slot_source(slot_ids, prompt_lengths, PAGE)
    target = stored_row(source, per_device, seq_count)
    empty_cache = jnp.zeros((SLOT_DEV, kv_width), jnp.bfloat16)
    key_piece = kv_piece[:, :kv_width]
    value_piece = kv_piece[:, kv_width:]
    piece_rows = key_piece.shape[0]
    found = is_live & (target >= 0) & (target < piece_rows)
    safe_index = jnp.clip(target, 0, piece_rows - 1)
    cache_keys = jnp.where(found[:, None], jnp.take(key_piece, safe_index, axis=0), empty_cache)
    cache_values = jnp.where(found[:, None], jnp.take(value_piece, safe_index, axis=0), empty_cache)
    return (normed, cache_keys, cache_values)


def solution(mesh):
    return jax.shard_map(
        body,
        mesh=mesh,
        in_specs=(
            P("seq", "tensor"),
            P("seq", "tensor"),
            P("seq", "tensor"),
            P("tensor", "seq"),
            P("seq", None),
            P(),
            P(),
        ),
        out_specs=(P("seq", None), P("seq", "tensor"), P("seq", "tensor")),
        check_vma=False,
    )
```

```python
import functools
import math

import jax
import jax.numpy as jnp
from jax import lax
from jax.experimental import pallas as pl
from jax.experimental.pallas import tpu as pltpu
from jax.sharding import PartitionSpec as P

HD = 128
PAGE = 128
SLOT_DEV = 704
MAX_PROMPT = 5120


def position_of(stored, per_device, devices):
    half_block = per_device // 2
    device = stored // per_device
    offset = stored % per_device
    return jnp.where(
        offset < half_block,
        device * half_block + offset,
        (2 * devices - 1 - device) * half_block + offset - half_block,
    )


def stored_row(position, per_device, devices):
    half_block = per_device // 2
    block_index = position // half_block
    device = jnp.where(block_index < devices, block_index, 2 * devices - 1 - block_index)
    offset = position % half_block + jnp.where(block_index < devices, 0, half_block)
    return device * per_device + offset


def segment_of(position, lengths):
    doc_ends = jnp.cumsum(lengths, dtype=jnp.int32)
    return jnp.sum(
        (position[:, None] >= doc_ends[None, :]).astype(jnp.int32), axis=1, dtype=jnp.int32
    )


def slot_source(slot_ids, lengths, page_size):
    padded = (lengths + page_size - 1) // page_size * page_size
    page_ends = jnp.cumsum(padded, dtype=jnp.int32)
    page_starts = page_ends - padded
    doc_ends = jnp.cumsum(lengths, dtype=jnp.int32)
    doc_starts = doc_ends - lengths
    before = (slot_ids[:, None] >= page_ends[None, :]).astype(jnp.int32)
    inside = (slot_ids[:, None] >= page_starts[None, :]).astype(jnp.int32) - before
    page_start = jnp.sum(before * padded[None, :], axis=1, dtype=jnp.int32)
    doc_start = jnp.sum(before * lengths[None, :], axis=1, dtype=jnp.int32)
    length = jnp.sum(inside * lengths[None, :], axis=1, dtype=jnp.int32)
    within = slot_ids - page_start
    is_live = within < length
    return (doc_start + within, is_live)


def attn_kernel(q_ref, kv_ref, qpos_ref, qseg_ref, kpos_ref, kseg_ref, o_ref, *, heads, scale):
    allowed = (kpos_ref[0] <= qpos_ref[0]) & (kseg_ref[0] == qseg_ref[0])
    key = kv_ref[0, :, :HD]
    value = kv_ref[0, :, HD:]
    for h in range(heads):
        query = q_ref[0, :, h * HD:(h + 1) * HD]
        scores = lax.dot_general(query, key, (((1,), (1,)), ((), ())),
                                 preferred_element_type=jnp.float32) * scale
        scores = jnp.where(allowed, scores, -1e30)
        top = jnp.max(scores, axis=1, keepdims=True)
        weights = jnp.where(allowed, jnp.exp(scores - top), 0.0)
        total = jnp.sum(weights, axis=1, keepdims=True)
        summed = jnp.dot(weights.astype(jnp.bfloat16), value, preferred_element_type=jnp.float32)
        o_ref[0, :, h * HD:(h + 1) * HD] = (summed / total).astype(o_ref.dtype)

def attend(q, kv, qpos, qseg, kpos, kseg):
    blocks, rows, width = q.shape
    window = kv.shape[1]
    heads = width // HD
    kern = functools.partial(attn_kernel, heads=heads, scale=1.0 / math.sqrt(HD))
    return pl.pallas_call(
        kern,
        grid=(blocks,),
        in_specs=[
            pl.BlockSpec((1, rows, width), lambda b: (b, 0, 0)),
            pl.BlockSpec((1, window, 2 * HD), lambda b: (b, 0, 0)),
            pl.BlockSpec((1, rows, 1), lambda b: (b, 0, 0)),
            pl.BlockSpec((1, rows, 1), lambda b: (b, 0, 0)),
            pl.BlockSpec((1, 1, window), lambda b: (b, 0, 0)),
            pl.BlockSpec((1, 1, window), lambda b: (b, 0, 0)),
        ],
        out_specs=pl.BlockSpec((1, rows, width), lambda b: (b, 0, 0)),
        out_shape=jax.ShapeDtypeStruct((blocks, rows, width), jnp.bfloat16),
        compiler_params=pltpu.CompilerParams(vmem_limit_bytes=48 * 1024 * 1024),
        cost_estimate=pl.CostEstimate(flops=4 * blocks * heads * rows * window * HD,
                                      transcendentals=blocks * heads * rows * window,
                                      bytes_accessed=blocks * (window * 2 * HD * 2 + 2 * rows * width * 2)),
    )(q, kv, qpos, qseg, kpos, kseg)

def norm_kernel(projected_ref, residual_ref, gain_ref, out_ref):
    hidden = residual_ref[...].astype(jnp.float32) + projected_ref[...].astype(jnp.float32)
    mean_square = jnp.mean(hidden * hidden, axis=-1, keepdims=True)
    out_ref[...] = (
        hidden * lax.rsqrt(mean_square + 1e-05) * gain_ref[...].astype(jnp.float32)
    ).astype(out_ref.dtype)


def residual_norm(projected, residual, gain, rows_per_step=40):
    rows, width = projected.shape
    steps = rows // rows_per_step
    return pl.pallas_call(
        norm_kernel,
        grid=(steps,),
        in_specs=[
            pl.BlockSpec((rows_per_step, width), lambda i: (i, 0)),
            pl.BlockSpec((rows_per_step, width), lambda i: (i, 0)),
            pl.BlockSpec((1, width), lambda i: (0, 0)),
        ],
        out_specs=pl.BlockSpec((rows_per_step, width), lambda i: (i, 0)),
        out_shape=jax.ShapeDtypeStruct((rows, width), jnp.bfloat16),
        cost_estimate=pl.CostEstimate(
            flops=5 * rows * width, transcendentals=rows, bytes_accessed=6 * rows * width
        ),
    )(projected, residual, gain.reshape(1, width))


def pair_then_ring_sum(partial):
    half_cols = partial.shape[1] // 2
    core = lax.axis_index("tc")
    swap = [(0, 1), (1, 0)]
    mine = lax.dynamic_slice_in_dim(partial, core * half_cols, half_cols, axis=1)
    other = lax.dynamic_slice_in_dim(partial, (1 - core) * half_cols, half_cols, axis=1)
    received = lax.ppermute(other, "tc", swap)
    pair = (mine.astype(jnp.float32) + received.astype(jnp.float32)).astype(jnp.bfloat16)
    reduced = lax.psum(pair, "ty")
    partner = lax.ppermute(reduced, "tc", swap)
    first = jnp.where(core == 0, reduced, partner)
    second = jnp.where(core == 0, partner, reduced)
    return jnp.concatenate([first, second], axis=1)


def body(queries, key_rows, value_rows, out_weight, residual_in, norm_gain, prompt_lengths):
    seq_count = lax.axis_size("seq")
    seq_index = lax.axis_index("seq")
    per_device = queries.shape[0]
    half = per_device // 2
    kv_width = key_rows.shape[1]
    kv_rows = jnp.concatenate([key_rows, value_rows], axis=1)
    stacked = lax.all_gather(
        jnp.concatenate([kv_rows, out_weight], axis=0), "seq", axis=1, tiled=True
    )
    weight_full = stacked[per_device:]
    kv_stored = jnp.transpose(
        stacked[:per_device].reshape(per_device, seq_count, 2 * kv_width), (1, 0, 2)
    )
    kv_piece = kv_stored.reshape(seq_count * per_device, 2 * kv_width)
    halves = kv_stored.reshape(seq_count, 2, half, 2 * kv_width)
    kv_pos = jnp.concatenate([halves[:, 0], halves[::-1, 1]], axis=0).reshape(
        seq_count * per_device, 2 * kv_width
    )
    window = min(seq_count * per_device, -(-(MAX_PROMPT - 1 + half) // 128) * 128)
    block_index = jnp.stack([seq_index, 2 * seq_count - 1 - seq_index])
    starts = jnp.clip(block_index * half + half - window, 0, seq_count * per_device - window)
    kv_win = jnp.stack(
        [lax.dynamic_slice_in_dim(kv_pos, starts[i], window, axis=0) for i in range(2)]
    )
    key_position = starts[:, None] + jnp.arange(window, dtype=jnp.int32)[None, :]
    query_position = block_index[:, None] * half + jnp.arange(half, dtype=jnp.int32)[None, :]
    key_segment = segment_of(key_position.reshape(-1), prompt_lengths).reshape(2, 1, window)
    query_segment = segment_of(query_position.reshape(-1), prompt_lengths).reshape(2, half, 1)
    attended = attend(
        queries.reshape(2, half, queries.shape[1]),
        kv_win,
        query_position[:, :, None],
        query_segment,
        key_position[:, None, :],
        key_segment,
    ).reshape(per_device, -1)
    partial_value = jnp.dot(attended, weight_full, preferred_element_type=jnp.float32)
    projected = pair_then_ring_sum(partial_value.astype(jnp.bfloat16))
    normed = residual_norm(projected, residual_in, norm_gain)
    slot_ids = seq_index * SLOT_DEV + jnp.arange(SLOT_DEV, dtype=jnp.int32)
    source, is_live = slot_source(slot_ids, prompt_lengths, PAGE)
    target = stored_row(source, per_device, seq_count)
    empty_cache = jnp.zeros((SLOT_DEV, kv_width), jnp.bfloat16)
    key_piece = kv_piece[:, :kv_width]
    value_piece = kv_piece[:, kv_width:]
    piece_rows = key_piece.shape[0]
    found = is_live & (target >= 0) & (target < piece_rows)
    safe_index = jnp.clip(target, 0, piece_rows - 1)
    cache_keys = jnp.where(found[:, None], jnp.take(key_piece, safe_index, axis=0), empty_cache)
    cache_values = jnp.where(found[:, None], jnp.take(value_piece, safe_index, axis=0), empty_cache)
    return (normed, cache_keys, cache_values)


def solution(mesh):
    seq_count, tensor_count = mesh.devices.shape
    split = jax.sharding.Mesh(
        mesh.devices.reshape(seq_count, tensor_count // 2, 2), ("seq", "ty", "tc")
    )
    tensor = ("ty", "tc")
    return jax.shard_map(
        body,
        mesh=split,
        in_specs=(
            P("seq", tensor),
            P("seq", tensor),
            P("seq", tensor),
            P(tensor, "seq"),
            P("seq", None),
            P(),
            P(),
        ),
        out_specs=(P("seq", None), P("seq", tensor), P("seq", tensor)),
        check_vma=False,
    )
```

```python
import functools
import math

import jax
import jax.numpy as jnp
from jax import lax
from jax.experimental import pallas as pl
from jax.experimental.pallas import tpu as pltpu
from jax.sharding import PartitionSpec as P

HD = 128
PAGE = 128
SLOT_DEV = 704
MAX_PROMPT = 5120


def position_of(stored, per_device, devices):
    half_block = per_device // 2
    device = stored // per_device
    offset = stored % per_device
    return jnp.where(
        offset < half_block,
        device * half_block + offset,
        (2 * devices - 1 - device) * half_block + offset - half_block,
    )


def stored_row(position, per_device, devices):
    half_block = per_device // 2
    block_index = position // half_block
    device = jnp.where(block_index < devices, block_index, 2 * devices - 1 - block_index)
    offset = position % half_block + jnp.where(block_index < devices, 0, half_block)
    return device * per_device + offset


def segment_of(position, lengths):
    doc_ends = jnp.cumsum(lengths, dtype=jnp.int32)
    return jnp.sum(
        (position[:, None] >= doc_ends[None, :]).astype(jnp.int32), axis=1, dtype=jnp.int32
    )


def slot_source(slot_ids, lengths, page_size):
    padded = (lengths + page_size - 1) // page_size * page_size
    page_ends = jnp.cumsum(padded, dtype=jnp.int32)
    page_starts = page_ends - padded
    doc_ends = jnp.cumsum(lengths, dtype=jnp.int32)
    doc_starts = doc_ends - lengths
    before = (slot_ids[:, None] >= page_ends[None, :]).astype(jnp.int32)
    inside = (slot_ids[:, None] >= page_starts[None, :]).astype(jnp.int32) - before
    page_start = jnp.sum(before * padded[None, :], axis=1, dtype=jnp.int32)
    doc_start = jnp.sum(before * lengths[None, :], axis=1, dtype=jnp.int32)
    length = jnp.sum(inside * lengths[None, :], axis=1, dtype=jnp.int32)
    within = slot_ids - page_start
    is_live = within < length
    return (doc_start + within, is_live)


def attn_kernel(
    first_ref, q_ref, g_hbm, qpos_ref, qseg_ref, kpos_ref, kseg_ref, o_ref, window, sems,
    *, heads, scale, blocks, half, seq_count, kv_cols,
):
    first = first_ref[pl.program_id(0)]
    copies = []
    for k in range(blocks):
        block = first + k
        upper = block >= seq_count
        row = jnp.where(upper, half, 0)
        device = jnp.where(upper, 2 * seq_count - 1 - block, block)
        copy = pltpu.make_async_copy(
            g_hbm.at[pl.ds(row, half), pl.ds(device * kv_cols, kv_cols)],
            window.at[pl.ds(k * half, half)],
            sems.at[k],
        )
        copy.start()
        copies.append(copy)
    pad = window.shape[0] - blocks * half
    if pad:
        window[pl.ds(blocks * half, pad), :] = jnp.zeros((pad, kv_cols), window.dtype)
    for copy in copies:
        copy.wait()
    allowed = (kpos_ref[0] <= qpos_ref[0]) & (kseg_ref[0] == qseg_ref[0])
    key = window[:, :HD]
    value = window[:, HD:]
    for h in range(heads):
        query = q_ref[0, :, h * HD:(h + 1) * HD]
        scores = lax.dot_general(
            query, key, (((1,), (1,)), ((), ())), preferred_element_type=jnp.float32
        ) * scale
        scores = jnp.where(allowed, scores, -1e30)
        top = jnp.max(scores, axis=1, keepdims=True)
        weights = jnp.where(allowed, jnp.exp(scores - top), 0.0)
        total = jnp.sum(weights, axis=1, keepdims=True)
        summed = jnp.dot(weights.astype(jnp.bfloat16), value, preferred_element_type=jnp.float32)
        o_ref[0, :, h * HD:(h + 1) * HD] = (summed / total).astype(o_ref.dtype)


def attend(first, q, gathered, qpos, qseg, kpos, kseg, blocks, seq_count, kv_cols):
    count, rows, width = q.shape
    window_rows = kpos.shape[-1]
    heads = width // HD
    kern = functools.partial(
        attn_kernel, heads=heads, scale=1.0 / math.sqrt(HD), blocks=blocks, half=rows,
        seq_count=seq_count, kv_cols=kv_cols,
    )
    grid_spec = pltpu.PrefetchScalarGridSpec(
        num_scalar_prefetch=1,
        grid=(count,),
        in_specs=[
            pl.BlockSpec((1, rows, width), lambda b, f: (b, 0, 0)),
            pl.BlockSpec(memory_space=pl.ANY),
            pl.BlockSpec((1, rows, 1), lambda b, f: (b, 0, 0)),
            pl.BlockSpec((1, rows, 1), lambda b, f: (b, 0, 0)),
            pl.BlockSpec((1, 1, window_rows), lambda b, f: (b, 0, 0)),
            pl.BlockSpec((1, 1, window_rows), lambda b, f: (b, 0, 0)),
        ],
        out_specs=pl.BlockSpec((1, rows, width), lambda b, f: (b, 0, 0)),
        scratch_shapes=[
            pltpu.VMEM((window_rows, kv_cols), gathered.dtype),
            pltpu.SemaphoreType.DMA((blocks,)),
        ],
    )
    return pl.pallas_call(
        kern,
        grid_spec=grid_spec,
        out_shape=jax.ShapeDtypeStruct((count, rows, width), jnp.bfloat16),
        compiler_params=pltpu.CompilerParams(vmem_limit_bytes=48 * 1024 * 1024),
        cost_estimate=pl.CostEstimate(
            flops=4 * count * heads * rows * window_rows * HD,
            transcendentals=count * heads * rows * window_rows,
            bytes_accessed=count * (window_rows * kv_cols * 2 + 2 * rows * width * 2),
        ),
    )(first, q, gathered, qpos, qseg, kpos, kseg)


def norm_kernel(projected_ref, residual_ref, gain_ref, out_ref):
    hidden = residual_ref[...].astype(jnp.float32) + projected_ref[...].astype(jnp.float32)
    mean_square = jnp.mean(hidden * hidden, axis=-1, keepdims=True)
    out_ref[...] = (
        hidden * lax.rsqrt(mean_square + 1e-05) * gain_ref[...].astype(jnp.float32)
    ).astype(out_ref.dtype)


def residual_norm(projected, residual, gain, rows_per_step=40):
    rows, width = projected.shape
    steps = rows // rows_per_step
    return pl.pallas_call(
        norm_kernel,
        grid=(steps,),
        in_specs=[
            pl.BlockSpec((rows_per_step, width), lambda i: (i, 0)),
            pl.BlockSpec((rows_per_step, width), lambda i: (i, 0)),
            pl.BlockSpec((1, width), lambda i: (0, 0)),
        ],
        out_specs=pl.BlockSpec((rows_per_step, width), lambda i: (i, 0)),
        out_shape=jax.ShapeDtypeStruct((rows, width), jnp.bfloat16),
        cost_estimate=pl.CostEstimate(
            flops=5 * rows * width, transcendentals=rows, bytes_accessed=6 * rows * width
        ),
    )(projected, residual, gain.reshape(1, width))


def body(queries, key_rows, value_rows, out_weight, residual_in, norm_gain, prompt_lengths):
    seq_count = lax.axis_size("seq")
    seq_index = lax.axis_index("seq")
    per_device = queries.shape[0]
    half = per_device // 2
    kv_width = key_rows.shape[1]
    kv_rows = jnp.concatenate([key_rows, value_rows], axis=1)
    stacked = lax.all_gather(
        jnp.concatenate([kv_rows, out_weight], axis=0), "seq", axis=1, tiled=True
    )
    weight_full = stacked[per_device:]
    kv_stored = jnp.transpose(
        stacked[:per_device].reshape(per_device, seq_count, 2 * kv_width), (1, 0, 2)
    )
    kv_piece = kv_stored.reshape(seq_count * per_device, 2 * kv_width)
    blocks = min(2 * seq_count, -(-(MAX_PROMPT - 1) // half) + 1)
    window = -(-(blocks * half) // 128) * 128
    block_index = jnp.stack([seq_index, 2 * seq_count - 1 - seq_index])
    first = jnp.clip(block_index - (blocks - 1), 0, 2 * seq_count - blocks).astype(jnp.int32)
    offsets = jnp.arange(window, dtype=jnp.int32)[None, :]
    key_position = jnp.where(
        offsets < blocks * half, first[:, None] * half + offsets, 4 * seq_count * per_device
    )
    query_position = block_index[:, None] * half + jnp.arange(half, dtype=jnp.int32)[None, :]
    key_segment = segment_of(key_position.reshape(-1), prompt_lengths).reshape(2, 1, window)
    query_segment = segment_of(query_position.reshape(-1), prompt_lengths).reshape(2, half, 1)
    attended = attend(
        first,
        queries.reshape(2, half, queries.shape[1]),
        stacked,
        query_position[:, :, None],
        query_segment,
        key_position[:, None, :],
        key_segment,
        blocks,
        seq_count,
        2 * kv_width,
    ).reshape(per_device, -1)
    partial_value = jnp.dot(attended, weight_full, preferred_element_type=jnp.float32)
    projected = lax.psum(partial_value.astype(jnp.bfloat16), "tensor")
    normed = residual_norm(projected, residual_in, norm_gain)
    slot_ids = seq_index * SLOT_DEV + jnp.arange(SLOT_DEV, dtype=jnp.int32)
    source, is_live = slot_source(slot_ids, prompt_lengths, PAGE)
    target = stored_row(source, per_device, seq_count)
    empty_cache = jnp.zeros((SLOT_DEV, kv_width), jnp.bfloat16)
    key_piece = kv_piece[:, :kv_width]
    value_piece = kv_piece[:, kv_width:]
    piece_rows = key_piece.shape[0]
    found = is_live & (target >= 0) & (target < piece_rows)
    safe_index = jnp.clip(target, 0, piece_rows - 1)
    cache_keys = jnp.where(found[:, None], jnp.take(key_piece, safe_index, axis=0), empty_cache)
    cache_values = jnp.where(found[:, None], jnp.take(value_piece, safe_index, axis=0), empty_cache)
    return (normed, cache_keys, cache_values)


def solution(mesh):
    return jax.shard_map(
        body,
        mesh=mesh,
        in_specs=(
            P("seq", "tensor"),
            P("seq", "tensor"),
            P("seq", "tensor"),
            P("tensor", "seq"),
            P("seq", None),
            P(),
            P(),
        ),
        out_specs=(P("seq", None), P("seq", "tensor"), P("seq", "tensor")),
        check_vma=False,
    )
```

```python
import functools
import math

import jax
import jax.numpy as jnp
from jax import lax
from jax.experimental import pallas as pl
from jax.experimental.pallas import tpu as pltpu
from jax.sharding import PartitionSpec as P

HD = 128
PAGE = 128
SLOT_DEV = 704
MAX_PROMPT = 5120


def position_of(stored, per_device, devices):
    half_block = per_device // 2
    device = stored // per_device
    offset = stored % per_device
    return jnp.where(
        offset < half_block,
        device * half_block + offset,
        (2 * devices - 1 - device) * half_block + offset - half_block,
    )


def stored_row(position, per_device, devices):
    half_block = per_device // 2
    block_index = position // half_block
    device = jnp.where(block_index < devices, block_index, 2 * devices - 1 - block_index)
    offset = position % half_block + jnp.where(block_index < devices, 0, half_block)
    return device * per_device + offset


def segment_of(position, lengths):
    doc_ends = jnp.cumsum(lengths, dtype=jnp.int32)
    return jnp.sum(
        (position[:, None] >= doc_ends[None, :]).astype(jnp.int32), axis=1, dtype=jnp.int32
    )


def slot_source(slot_ids, lengths, page_size):
    padded = (lengths + page_size - 1) // page_size * page_size
    page_ends = jnp.cumsum(padded, dtype=jnp.int32)
    page_starts = page_ends - padded
    doc_ends = jnp.cumsum(lengths, dtype=jnp.int32)
    doc_starts = doc_ends - lengths
    before = (slot_ids[:, None] >= page_ends[None, :]).astype(jnp.int32)
    inside = (slot_ids[:, None] >= page_starts[None, :]).astype(jnp.int32) - before
    page_start = jnp.sum(before * padded[None, :], axis=1, dtype=jnp.int32)
    doc_start = jnp.sum(before * lengths[None, :], axis=1, dtype=jnp.int32)
    length = jnp.sum(inside * lengths[None, :], axis=1, dtype=jnp.int32)
    within = slot_ids - page_start
    is_live = within < length
    return (doc_start + within, is_live)


def attn_kernel(
    first_ref, q_ref, g_hbm, qpos_ref, qseg_ref, kpos_ref, kseg_ref, o_ref, window, sems,
    *, heads, scale, blocks, half, seq_count, kv_cols,
):
    first = first_ref[pl.program_id(0)]
    copies = []
    for k in range(blocks):
        block = first + k
        upper = block >= seq_count
        row = jnp.where(upper, half, 0)
        device = jnp.where(upper, 2 * seq_count - 1 - block, block)
        copy = pltpu.make_async_copy(
            g_hbm.at[pl.ds(row, half), pl.ds(device * kv_cols, kv_cols)],
            window.at[pl.ds(k * half, half)],
            sems.at[k],
        )
        copy.start()
        copies.append(copy)
    pad = window.shape[0] - blocks * half
    if pad:
        window[pl.ds(blocks * half, pad), :] = jnp.zeros((pad, kv_cols), window.dtype)
    for copy in copies:
        copy.wait()
    allowed = (kpos_ref[0] <= qpos_ref[0]) & (kseg_ref[0] == qseg_ref[0])
    key = window[:, :HD]
    value = window[:, HD:]
    for h in range(heads):
        query = q_ref[0, :, h * HD:(h + 1) * HD]
        scores = lax.dot_general(
            query, key, (((1,), (1,)), ((), ())), preferred_element_type=jnp.float32
        ) * scale
        scores = jnp.where(allowed, scores, -1e30)
        top = jnp.max(scores, axis=1, keepdims=True)
        weights = jnp.where(allowed, jnp.exp(scores - top), 0.0)
        total = jnp.sum(weights, axis=1, keepdims=True)
        summed = jnp.dot(weights.astype(jnp.bfloat16), value, preferred_element_type=jnp.float32)
        o_ref[0, :, h * HD:(h + 1) * HD] = (summed / total).astype(o_ref.dtype)


def attend(first, q, gathered, qpos, qseg, kpos, kseg, blocks, seq_count, kv_cols):
    count, rows, width = q.shape
    window_rows = kpos.shape[-1]
    heads = width // HD
    kern = functools.partial(
        attn_kernel, heads=heads, scale=1.0 / math.sqrt(HD), blocks=blocks, half=rows,
        seq_count=seq_count, kv_cols=kv_cols,
    )
    grid_spec = pltpu.PrefetchScalarGridSpec(
        num_scalar_prefetch=1,
        grid=(count,),
        in_specs=[
            pl.BlockSpec((1, rows, width), lambda b, f: (b, 0, 0)),
            pl.BlockSpec(memory_space=pl.ANY),
            pl.BlockSpec((1, rows, 1), lambda b, f: (b, 0, 0)),
            pl.BlockSpec((1, rows, 1), lambda b, f: (b, 0, 0)),
            pl.BlockSpec((1, 1, window_rows), lambda b, f: (b, 0, 0)),
            pl.BlockSpec((1, 1, window_rows), lambda b, f: (b, 0, 0)),
        ],
        out_specs=pl.BlockSpec((1, rows, width), lambda b, f: (b, 0, 0)),
        scratch_shapes=[
            pltpu.VMEM((window_rows, kv_cols), gathered.dtype),
            pltpu.SemaphoreType.DMA((blocks,)),
        ],
    )
    return pl.pallas_call(
        kern,
        grid_spec=grid_spec,
        out_shape=jax.ShapeDtypeStruct((count, rows, width), jnp.bfloat16),
        compiler_params=pltpu.CompilerParams(vmem_limit_bytes=48 * 1024 * 1024),
        cost_estimate=pl.CostEstimate(
            flops=4 * count * heads * rows * window_rows * HD,
            transcendentals=count * heads * rows * window_rows,
            bytes_accessed=count * (window_rows * kv_cols * 2 + 2 * rows * width * 2),
        ),
    )(first, q, gathered, qpos, qseg, kpos, kseg)


def norm_kernel(projected_ref, residual_ref, gain_ref, out_ref):
    hidden = residual_ref[...].astype(jnp.float32) + projected_ref[...].astype(jnp.float32)
    mean_square = jnp.mean(hidden * hidden, axis=-1, keepdims=True)
    out_ref[...] = (
        hidden * lax.rsqrt(mean_square + 1e-05) * gain_ref[...].astype(jnp.float32)
    ).astype(out_ref.dtype)


def residual_norm(projected, residual, gain, rows_per_step=40):
    rows, width = projected.shape
    steps = rows // rows_per_step
    return pl.pallas_call(
        norm_kernel,
        grid=(steps,),
        in_specs=[
            pl.BlockSpec((rows_per_step, width), lambda i: (i, 0)),
            pl.BlockSpec((rows_per_step, width), lambda i: (i, 0)),
            pl.BlockSpec((1, width), lambda i: (0, 0)),
        ],
        out_specs=pl.BlockSpec((rows_per_step, width), lambda i: (i, 0)),
        out_shape=jax.ShapeDtypeStruct((rows, width), jnp.bfloat16),
        cost_estimate=pl.CostEstimate(
            flops=5 * rows * width, transcendentals=rows, bytes_accessed=6 * rows * width
        ),
    )(projected, residual, gain.reshape(1, width))


def body(queries, key_rows, value_rows, out_weight, residual_in, norm_gain, prompt_lengths):
    seq_count = lax.axis_size("seq")
    seq_index = lax.axis_index("seq")
    per_device = queries.shape[0]
    half = per_device // 2
    kv_width = key_rows.shape[1]
    kv_rows = jnp.concatenate([key_rows, value_rows], axis=1)
    stacked = lax.all_gather(
        jnp.concatenate([kv_rows, out_weight], axis=0), "seq", axis=1, tiled=True
    )
    weight_full = stacked[per_device:]
    blocks = min(2 * seq_count, -(-(MAX_PROMPT - 1) // half) + 1)
    window = -(-(blocks * half) // 128) * 128
    block_index = jnp.stack([seq_index, 2 * seq_count - 1 - seq_index])
    first = jnp.clip(block_index - (blocks - 1), 0, 2 * seq_count - blocks).astype(jnp.int32)
    offsets = jnp.arange(window, dtype=jnp.int32)[None, :]
    key_position = jnp.where(
        offsets < blocks * half, first[:, None] * half + offsets, 4 * seq_count * per_device
    )
    query_position = block_index[:, None] * half + jnp.arange(half, dtype=jnp.int32)[None, :]
    key_segment = segment_of(key_position.reshape(-1), prompt_lengths).reshape(2, 1, window)
    query_segment = segment_of(query_position.reshape(-1), prompt_lengths).reshape(2, half, 1)
    attended = attend(
        first,
        queries.reshape(2, half, queries.shape[1]),
        stacked,
        query_position[:, :, None],
        query_segment,
        key_position[:, None, :],
        key_segment,
        blocks,
        seq_count,
        2 * kv_width,
    ).reshape(per_device, -1)
    partial_value = jnp.dot(attended, weight_full, preferred_element_type=jnp.float32)
    partial_value, stacked = lax.optimization_barrier((partial_value.astype(jnp.bfloat16), stacked))
    projected = lax.psum(partial_value, "tensor")
    normed = residual_norm(projected, residual_in, norm_gain)
    slot_ids = seq_index * SLOT_DEV + jnp.arange(SLOT_DEV, dtype=jnp.int32)
    source, is_live = slot_source(slot_ids, prompt_lengths, PAGE)
    target = stored_row(source, per_device, seq_count)
    empty_cache = jnp.zeros((SLOT_DEV, kv_width), jnp.bfloat16)
    kv_grid = stacked[:per_device].reshape(per_device, seq_count, 2 * kv_width)
    piece_rows = seq_count * per_device
    found = is_live & (target >= 0) & (target < piece_rows)
    safe_index = jnp.clip(target, 0, piece_rows - 1)
    cache_rows = kv_grid[safe_index % per_device, safe_index // per_device]
    cache_keys = jnp.where(found[:, None], cache_rows[:, :kv_width], empty_cache)
    cache_values = jnp.where(found[:, None], cache_rows[:, kv_width:], empty_cache)
    return (normed, cache_keys, cache_values)


def solution(mesh):
    return jax.shard_map(
        body,
        mesh=mesh,
        in_specs=(
            P("seq", "tensor"),
            P("seq", "tensor"),
            P("seq", "tensor"),
            P("tensor", "seq"),
            P("seq", None),
            P(),
            P(),
        ),
        out_specs=(P("seq", None), P("seq", "tensor"), P("seq", "tensor")),
        check_vma=False,
    )
```

```python
import functools
import math

import jax
import jax.numpy as jnp
from jax import lax
from jax.experimental import pallas as pl
from jax.experimental.pallas import tpu as pltpu
from jax.sharding import PartitionSpec as P

HD = 128
PAGE = 128
SLOT_DEV = 704
MAX_PROMPT = 5120


def position_of(stored, per_device, devices):
    half_block = per_device // 2
    device = stored // per_device
    offset = stored % per_device
    return jnp.where(
        offset < half_block,
        device * half_block + offset,
        (2 * devices - 1 - device) * half_block + offset - half_block,
    )


def stored_row(position, per_device, devices):
    half_block = per_device // 2
    block_index = position // half_block
    device = jnp.where(block_index < devices, block_index, 2 * devices - 1 - block_index)
    offset = position % half_block + jnp.where(block_index < devices, 0, half_block)
    return device * per_device + offset


def segment_of(position, lengths):
    doc_ends = jnp.cumsum(lengths, dtype=jnp.int32)
    return jnp.sum(
        (position[:, None] >= doc_ends[None, :]).astype(jnp.int32), axis=1, dtype=jnp.int32
    )


def slot_source(slot_ids, lengths, page_size):
    padded = (lengths + page_size - 1) // page_size * page_size
    page_ends = jnp.cumsum(padded, dtype=jnp.int32)
    page_starts = page_ends - padded
    doc_ends = jnp.cumsum(lengths, dtype=jnp.int32)
    doc_starts = doc_ends - lengths
    before = (slot_ids[:, None] >= page_ends[None, :]).astype(jnp.int32)
    inside = (slot_ids[:, None] >= page_starts[None, :]).astype(jnp.int32) - before
    page_start = jnp.sum(before * padded[None, :], axis=1, dtype=jnp.int32)
    doc_start = jnp.sum(before * lengths[None, :], axis=1, dtype=jnp.int32)
    length = jnp.sum(inside * lengths[None, :], axis=1, dtype=jnp.int32)
    within = slot_ids - page_start
    is_live = within < length
    return (doc_start + within, is_live)


def attn_kernel(
    first_ref, q_ref, g_hbm, qpos_ref, qseg_ref, kpos_ref, kseg_ref, o_ref, window, sems,
    weight, weight_sem, attended, *, heads, scale, blocks, half, seq_count, kv_cols, weight_row,
):
    step = pl.program_id(0)
    first = first_ref[step]
    weight_copy = pltpu.make_async_copy(
        g_hbm.at[pl.ds(weight_row, weight.shape[0])], weight, weight_sem.at[0]
    )

    @pl.when(step == 0)
    def _():
        weight_copy.start()

    copies = []
    for k in range(blocks):
        block = first + k
        upper = block >= seq_count
        row = jnp.where(upper, half, 0)
        device = jnp.where(upper, 2 * seq_count - 1 - block, block)
        copy = pltpu.make_async_copy(
            g_hbm.at[pl.ds(row, half), pl.ds(device * kv_cols, kv_cols)],
            window.at[pl.ds(k * half, half)],
            sems.at[k],
        )
        copy.start()
        copies.append(copy)
    pad = window.shape[0] - blocks * half
    if pad:
        window[pl.ds(blocks * half, pad), :] = jnp.zeros((pad, kv_cols), window.dtype)
    for copy in copies:
        copy.wait()
    allowed = (kpos_ref[0] <= qpos_ref[0]) & (kseg_ref[0] == qseg_ref[0])
    key = window[:, :HD]
    value = window[:, HD:]
    for h in range(heads):
        query = q_ref[0, :, h * HD:(h + 1) * HD]
        scores = lax.dot_general(
            query, key, (((1,), (1,)), ((), ())), preferred_element_type=jnp.float32
        ) * scale
        scores = jnp.where(allowed, scores, -1e30)
        top = jnp.max(scores, axis=1, keepdims=True)
        weights = jnp.where(allowed, jnp.exp(scores - top), 0.0)
        total = jnp.sum(weights, axis=1, keepdims=True)
        summed = jnp.dot(weights.astype(jnp.bfloat16), value, preferred_element_type=jnp.float32)
        attended[:, h * HD:(h + 1) * HD] = (summed / total).astype(attended.dtype)

    @pl.when(step == 0)
    def _():
        weight_copy.wait()

    out_cols = o_ref.shape[2]
    chunk = 1024 if out_cols % 1024 == 0 else out_cols
    for c in range(out_cols // chunk):
        o_ref[0, :, c * chunk:(c + 1) * chunk] = jnp.dot(
            attended[...], weight[:, c * chunk:(c + 1) * chunk], preferred_element_type=jnp.float32
        ).astype(o_ref.dtype)


def attend(first, q, gathered, qpos, qseg, kpos, kseg, blocks, seq_count, kv_cols):
    count, rows, width = q.shape
    window_rows = kpos.shape[-1]
    heads = width // HD
    weight_row = count * rows
    out_cols = gathered.shape[1]
    kern = functools.partial(
        attn_kernel, heads=heads, scale=1.0 / math.sqrt(HD), blocks=blocks, half=rows,
        seq_count=seq_count, kv_cols=kv_cols, weight_row=weight_row,
    )
    grid_spec = pltpu.PrefetchScalarGridSpec(
        num_scalar_prefetch=1,
        grid=(count,),
        in_specs=[
            pl.BlockSpec((1, rows, width), lambda b, f: (b, 0, 0)),
            pl.BlockSpec(memory_space=pl.ANY),
            pl.BlockSpec((1, rows, 1), lambda b, f: (b, 0, 0)),
            pl.BlockSpec((1, rows, 1), lambda b, f: (b, 0, 0)),
            pl.BlockSpec((1, 1, window_rows), lambda b, f: (b, 0, 0)),
            pl.BlockSpec((1, 1, window_rows), lambda b, f: (b, 0, 0)),
        ],
        out_specs=pl.BlockSpec((1, rows, out_cols), lambda b, f: (b, 0, 0)),
        scratch_shapes=[
            pltpu.VMEM((window_rows, kv_cols), gathered.dtype),
            pltpu.SemaphoreType.DMA((blocks,)),
            pltpu.VMEM((gathered.shape[0] - weight_row, out_cols), gathered.dtype),
            pltpu.SemaphoreType.DMA((1,)),
            pltpu.VMEM((rows, width), jnp.bfloat16),
        ],
    )
    return pl.pallas_call(
        kern,
        grid_spec=grid_spec,
        out_shape=jax.ShapeDtypeStruct((count, rows, out_cols), jnp.bfloat16),
        compiler_params=pltpu.CompilerParams(vmem_limit_bytes=56 * 1024 * 1024),
        cost_estimate=pl.CostEstimate(
            flops=4 * count * heads * rows * window_rows * HD + 2 * count * rows * width * out_cols,
            transcendentals=count * heads * rows * window_rows,
            bytes_accessed=count * (window_rows * kv_cols * 2 + rows * width * 2 + rows * out_cols * 2)
            + (gathered.shape[0] - weight_row) * out_cols * 2,
        ),
    )(first, q, gathered, qpos, qseg, kpos, kseg)


def norm_kernel(projected_ref, residual_ref, gain_ref, out_ref):
    hidden = residual_ref[...].astype(jnp.float32) + projected_ref[...].astype(jnp.float32)
    mean_square = jnp.mean(hidden * hidden, axis=-1, keepdims=True)
    out_ref[...] = (
        hidden * lax.rsqrt(mean_square + 1e-05) * gain_ref[...].astype(jnp.float32)
    ).astype(out_ref.dtype)


def residual_norm(projected, residual, gain, rows_per_step=40):
    rows, width = projected.shape
    steps = rows // rows_per_step
    return pl.pallas_call(
        norm_kernel,
        grid=(steps,),
        in_specs=[
            pl.BlockSpec((rows_per_step, width), lambda i: (i, 0)),
            pl.BlockSpec((rows_per_step, width), lambda i: (i, 0)),
            pl.BlockSpec((1, width), lambda i: (0, 0)),
        ],
        out_specs=pl.BlockSpec((rows_per_step, width), lambda i: (i, 0)),
        out_shape=jax.ShapeDtypeStruct((rows, width), jnp.bfloat16),
        cost_estimate=pl.CostEstimate(
            flops=5 * rows * width, transcendentals=rows, bytes_accessed=6 * rows * width
        ),
    )(projected, residual, gain.reshape(1, width))


def body(queries, key_rows, value_rows, out_weight, residual_in, norm_gain, prompt_lengths):
    seq_count = lax.axis_size("seq")
    seq_index = lax.axis_index("seq")
    per_device = queries.shape[0]
    half = per_device // 2
    kv_width = key_rows.shape[1]
    kv_rows = jnp.concatenate([key_rows, value_rows], axis=1)
    stacked = lax.all_gather(
        jnp.concatenate([kv_rows, out_weight], axis=0), "seq", axis=1, tiled=True
    )
    blocks = min(2 * seq_count, -(-(MAX_PROMPT - 1) // half) + 1)
    window = -(-(blocks * half) // 128) * 128
    block_index = jnp.stack([seq_index, 2 * seq_count - 1 - seq_index])
    first = jnp.clip(block_index - (blocks - 1), 0, 2 * seq_count - blocks).astype(jnp.int32)
    offsets = jnp.arange(window, dtype=jnp.int32)[None, :]
    key_position = jnp.where(
        offsets < blocks * half, first[:, None] * half + offsets, 4 * seq_count * per_device
    )
    query_position = block_index[:, None] * half + jnp.arange(half, dtype=jnp.int32)[None, :]
    key_segment = segment_of(key_position.reshape(-1), prompt_lengths).reshape(2, 1, window)
    query_segment = segment_of(query_position.reshape(-1), prompt_lengths).reshape(2, half, 1)
    partial_value = attend(
        first,
        queries.reshape(2, half, queries.shape[1]),
        stacked,
        query_position[:, :, None],
        query_segment,
        key_position[:, None, :],
        key_segment,
        blocks,
        seq_count,
        2 * kv_width,
    ).reshape(per_device, -1)
    partial_value, stacked = lax.optimization_barrier((partial_value, stacked))
    projected = lax.psum(partial_value, "tensor")
    normed = residual_norm(projected, residual_in, norm_gain)
    slot_ids = seq_index * SLOT_DEV + jnp.arange(SLOT_DEV, dtype=jnp.int32)
    source, is_live = slot_source(slot_ids, prompt_lengths, PAGE)
    target = stored_row(source, per_device, seq_count)
    empty_cache = jnp.zeros((SLOT_DEV, kv_width), jnp.bfloat16)
    kv_grid = stacked[:per_device].reshape(per_device, seq_count, 2 * kv_width)
    piece_rows = seq_count * per_device
    found = is_live & (target >= 0) & (target < piece_rows)
    safe_index = jnp.clip(target, 0, piece_rows - 1)
    cache_rows = kv_grid[safe_index % per_device, safe_index // per_device]
    cache_keys = jnp.where(found[:, None], cache_rows[:, :kv_width], empty_cache)
    cache_values = jnp.where(found[:, None], cache_rows[:, kv_width:], empty_cache)
    return (normed, cache_keys, cache_values)


def solution(mesh):
    return jax.shard_map(
        body,
        mesh=mesh,
        in_specs=(
            P("seq", "tensor"),
            P("seq", "tensor"),
            P("seq", "tensor"),
            P("tensor", "seq"),
            P("seq", None),
            P(),
            P(),
        ),
        out_specs=(P("seq", None), P("seq", "tensor"), P("seq", "tensor")),
        check_vma=False,
    )
```

```python
import functools
import math

import jax
import jax.numpy as jnp
from jax import lax
from jax.experimental import pallas as pl
from jax.experimental.pallas import tpu as pltpu
from jax.sharding import PartitionSpec as P

HD = 128
PAGE = 128
SLOT_DEV = 704
MAX_PROMPT = 5120


def position_of(stored, per_device, devices):
    half_block = per_device // 2
    device = stored // per_device
    offset = stored % per_device
    return jnp.where(
        offset < half_block,
        device * half_block + offset,
        (2 * devices - 1 - device) * half_block + offset - half_block,
    )


def stored_row(position, per_device, devices):
    half_block = per_device // 2
    block_index = position // half_block
    device = jnp.where(block_index < devices, block_index, 2 * devices - 1 - block_index)
    offset = position % half_block + jnp.where(block_index < devices, 0, half_block)
    return device * per_device + offset


def segment_of(position, lengths):
    doc_ends = jnp.cumsum(lengths, dtype=jnp.int32)
    return jnp.sum(
        (position[:, None] >= doc_ends[None, :]).astype(jnp.int32), axis=1, dtype=jnp.int32
    )


def slot_source(slot_ids, lengths, page_size):
    padded = (lengths + page_size - 1) // page_size * page_size
    page_ends = jnp.cumsum(padded, dtype=jnp.int32)
    page_starts = page_ends - padded
    doc_ends = jnp.cumsum(lengths, dtype=jnp.int32)
    doc_starts = doc_ends - lengths
    before = (slot_ids[:, None] >= page_ends[None, :]).astype(jnp.int32)
    inside = (slot_ids[:, None] >= page_starts[None, :]).astype(jnp.int32) - before
    page_start = jnp.sum(before * padded[None, :], axis=1, dtype=jnp.int32)
    doc_start = jnp.sum(before * lengths[None, :], axis=1, dtype=jnp.int32)
    length = jnp.sum(inside * lengths[None, :], axis=1, dtype=jnp.int32)
    within = slot_ids - page_start
    is_live = within < length
    return (doc_start + within, is_live)


def attn_kernel(
    first_ref, q_ref, g_hbm, qpos_ref, qseg_ref, kpos_ref, kseg_ref, o_ref, window, sems,
    weight, weight_sem, attended, *, heads, scale, blocks, half, seq_count, kv_cols, weight_row,
):
    step = pl.program_id(0)
    first = first_ref[step]
    weight_copy = pltpu.make_async_copy(
        g_hbm.at[pl.ds(weight_row, weight.shape[0])], weight, weight_sem.at[0]
    )

    @pl.when(step == 0)
    def _():
        weight_copy.start()

    copies = []
    for k in range(blocks):
        block = first + k
        upper = block >= seq_count
        row = jnp.where(upper, half, 0)
        device = jnp.where(upper, 2 * seq_count - 1 - block, block)
        copy = pltpu.make_async_copy(
            g_hbm.at[pl.ds(row, half), pl.ds(device * kv_cols, kv_cols)],
            window.at[pl.ds(k * half, half)],
            sems.at[k],
        )
        copy.start()
        copies.append(copy)
    pad = window.shape[0] - blocks * half
    if pad:
        window[pl.ds(blocks * half, pad), :] = jnp.zeros((pad, kv_cols), window.dtype)
    for copy in copies:
        copy.wait()
    allowed = (kpos_ref[0] <= qpos_ref[0]) & (kseg_ref[0] == qseg_ref[0])
    key = window[:, :HD]
    value = window[:, HD:]
    for h in range(heads):
        query = q_ref[0, :, h * HD:(h + 1) * HD]
        scores = lax.dot_general(
            query, key, (((1,), (1,)), ((), ())), preferred_element_type=jnp.float32
        ) * scale
        scores = jnp.where(allowed, scores, -1e30)
        top = jnp.max(scores, axis=1, keepdims=True)
        weights = jnp.where(allowed, jnp.exp(scores - top), 0.0)
        total = jnp.sum(weights, axis=1, keepdims=True)
        summed = jnp.dot(weights.astype(jnp.bfloat16), value, preferred_element_type=jnp.float32)
        attended[:, h * HD:(h + 1) * HD] = (summed / total).astype(attended.dtype)

    @pl.when(step == 0)
    def _():
        weight_copy.wait()

    out_cols = o_ref.shape[2]
    chunk = 1024 if out_cols % 1024 == 0 else out_cols
    for c in range(out_cols // chunk):
        o_ref[0, :, c * chunk:(c + 1) * chunk] = jnp.dot(
            attended[...], weight[:, c * chunk:(c + 1) * chunk], preferred_element_type=jnp.float32
        ).astype(o_ref.dtype)


def attend(first, q, gathered, qpos, qseg, kpos, kseg, blocks, seq_count, kv_cols):
    count, rows, width = q.shape
    window_rows = kpos.shape[-1]
    heads = width // HD
    weight_row = count * rows
    out_cols = gathered.shape[1]
    kern = functools.partial(
        attn_kernel, heads=heads, scale=1.0 / math.sqrt(HD), blocks=blocks, half=rows,
        seq_count=seq_count, kv_cols=kv_cols, weight_row=weight_row,
    )
    grid_spec = pltpu.PrefetchScalarGridSpec(
        num_scalar_prefetch=1,
        grid=(count,),
        in_specs=[
            pl.BlockSpec((1, rows, width), lambda b, f: (b, 0, 0)),
            pl.BlockSpec(memory_space=pl.ANY),
            pl.BlockSpec((1, rows, 1), lambda b, f: (b, 0, 0)),
            pl.BlockSpec((1, rows, 1), lambda b, f: (b, 0, 0)),
            pl.BlockSpec((1, 1, window_rows), lambda b, f: (b, 0, 0)),
            pl.BlockSpec((1, 1, window_rows), lambda b, f: (b, 0, 0)),
        ],
        out_specs=pl.BlockSpec((1, rows, out_cols), lambda b, f: (b, 0, 0)),
        scratch_shapes=[
            pltpu.VMEM((window_rows, kv_cols), gathered.dtype),
            pltpu.SemaphoreType.DMA((blocks,)),
            pltpu.VMEM((gathered.shape[0] - weight_row, out_cols), gathered.dtype),
            pltpu.SemaphoreType.DMA((1,)),
            pltpu.VMEM((rows, width), jnp.bfloat16),
        ],
    )
    return pl.pallas_call(
        kern,
        grid_spec=grid_spec,
        out_shape=jax.ShapeDtypeStruct((count, rows, out_cols), jnp.bfloat16),
        compiler_params=pltpu.CompilerParams(vmem_limit_bytes=56 * 1024 * 1024),
        cost_estimate=pl.CostEstimate(
            flops=4 * count * heads * rows * window_rows * HD + 2 * count * rows * width * out_cols,
            transcendentals=count * heads * rows * window_rows,
            bytes_accessed=count * (window_rows * kv_cols * 2 + rows * width * 2 + rows * out_cols * 2)
            + (gathered.shape[0] - weight_row) * out_cols * 2,
        ),
    )(first, q, gathered, qpos, qseg, kpos, kseg)


def norm_kernel(projected_ref, residual_ref, gain_ref, out_ref):
    hidden = residual_ref[...].astype(jnp.float32) + projected_ref[...].astype(jnp.float32)
    mean_square = jnp.mean(hidden * hidden, axis=-1, keepdims=True)
    out_ref[...] = (
        hidden * lax.rsqrt(mean_square + 1e-05) * gain_ref[...].astype(jnp.float32)
    ).astype(out_ref.dtype)


def residual_norm(projected, residual, gain, rows_per_step=80):
    rows, width = projected.shape
    steps = rows // rows_per_step
    return pl.pallas_call(
        norm_kernel,
        grid=(steps,),
        in_specs=[
            pl.BlockSpec((rows_per_step, width), lambda i: (i, 0)),
            pl.BlockSpec((rows_per_step, width), lambda i: (i, 0)),
            pl.BlockSpec((1, width), lambda i: (0, 0)),
        ],
        out_specs=pl.BlockSpec((rows_per_step, width), lambda i: (i, 0)),
        out_shape=jax.ShapeDtypeStruct((rows, width), jnp.bfloat16),
        cost_estimate=pl.CostEstimate(
            flops=5 * rows * width, transcendentals=rows, bytes_accessed=6 * rows * width
        ),
    )(projected, residual, gain.reshape(1, width))


def body(queries, key_rows, value_rows, out_weight, residual_in, norm_gain, prompt_lengths):
    seq_count = lax.axis_size("seq")
    seq_index = lax.axis_index("seq")
    per_device = queries.shape[0]
    half = per_device // 2
    kv_width = key_rows.shape[1]
    kv_rows = jnp.concatenate([key_rows, value_rows], axis=1)
    stacked = lax.all_gather(
        jnp.concatenate([kv_rows, out_weight], axis=0), "seq", axis=1, tiled=True
    )
    blocks = min(2 * seq_count, -(-(MAX_PROMPT - 1) // half) + 1)
    window = -(-(blocks * half) // 128) * 128
    block_index = jnp.stack([seq_index, 2 * seq_count - 1 - seq_index])
    first = jnp.clip(block_index - (blocks - 1), 0, 2 * seq_count - blocks).astype(jnp.int32)
    offsets = jnp.arange(window, dtype=jnp.int32)[None, :]
    key_position = jnp.where(
        offsets < blocks * half, first[:, None] * half + offsets, 4 * seq_count * per_device
    )
    query_position = block_index[:, None] * half + jnp.arange(half, dtype=jnp.int32)[None, :]
    key_segment = segment_of(key_position.reshape(-1), prompt_lengths).reshape(2, 1, window)
    query_segment = segment_of(query_position.reshape(-1), prompt_lengths).reshape(2, half, 1)
    partial_value = attend(
        first,
        queries.reshape(2, half, queries.shape[1]),
        stacked,
        query_position[:, :, None],
        query_segment,
        key_position[:, None, :],
        key_segment,
        blocks,
        seq_count,
        2 * kv_width,
    ).reshape(per_device, -1)
    partial_value, stacked = lax.optimization_barrier((partial_value, stacked))
    projected = lax.psum(partial_value, "tensor")
    normed = residual_norm(projected, residual_in, norm_gain)
    slot_ids = seq_index * SLOT_DEV + jnp.arange(SLOT_DEV, dtype=jnp.int32)
    source, is_live = slot_source(slot_ids, prompt_lengths, PAGE)
    target = stored_row(source, per_device, seq_count)
    empty_cache = jnp.zeros((SLOT_DEV, kv_width), jnp.bfloat16)
    kv_grid = stacked[:per_device].reshape(per_device, seq_count, 2 * kv_width)
    piece_rows = seq_count * per_device
    found = is_live & (target >= 0) & (target < piece_rows)
    safe_index = jnp.clip(target, 0, piece_rows - 1)
    cache_rows = kv_grid[safe_index % per_device, safe_index // per_device]
    cache_keys = jnp.where(found[:, None], cache_rows[:, :kv_width], empty_cache)
    cache_values = jnp.where(found[:, None], cache_rows[:, kv_width:], empty_cache)
    return (normed, cache_keys, cache_values)


def solution(mesh):
    return jax.shard_map(
        body,
        mesh=mesh,
        in_specs=(
            P("seq", "tensor"),
            P("seq", "tensor"),
            P("seq", "tensor"),
            P("tensor", "seq"),
            P("seq", None),
            P(),
            P(),
        ),
        out_specs=(P("seq", None), P("seq", "tensor"), P("seq", "tensor")),
        check_vma=False,
    )
```

```python
import functools
import math

import jax
import jax.numpy as jnp
from jax import lax
from jax.experimental import pallas as pl
from jax.experimental.pallas import tpu as pltpu
from jax.sharding import PartitionSpec as P

HD = 128
PAGE = 128
SLOT_DEV = 704
MAX_PROMPT = 5120


def position_of(stored, per_device, devices):
    half_block = per_device // 2
    device = stored // per_device
    offset = stored % per_device
    return jnp.where(
        offset < half_block,
        device * half_block + offset,
        (2 * devices - 1 - device) * half_block + offset - half_block,
    )


def stored_row(position, per_device, devices):
    half_block = per_device // 2
    block_index = position // half_block
    device = jnp.where(block_index < devices, block_index, 2 * devices - 1 - block_index)
    offset = position % half_block + jnp.where(block_index < devices, 0, half_block)
    return device * per_device + offset


def segment_of(position, lengths):
    doc_ends = jnp.cumsum(lengths, dtype=jnp.int32)
    return jnp.sum(
        (position[:, None] >= doc_ends[None, :]).astype(jnp.int32), axis=1, dtype=jnp.int32
    )


def slot_source(slot_ids, lengths, page_size):
    padded = (lengths + page_size - 1) // page_size * page_size
    page_ends = jnp.cumsum(padded, dtype=jnp.int32)
    page_starts = page_ends - padded
    doc_ends = jnp.cumsum(lengths, dtype=jnp.int32)
    doc_starts = doc_ends - lengths
    before = (slot_ids[:, None] >= page_ends[None, :]).astype(jnp.int32)
    inside = (slot_ids[:, None] >= page_starts[None, :]).astype(jnp.int32) - before
    page_start = jnp.sum(before * padded[None, :], axis=1, dtype=jnp.int32)
    doc_start = jnp.sum(before * lengths[None, :], axis=1, dtype=jnp.int32)
    length = jnp.sum(inside * lengths[None, :], axis=1, dtype=jnp.int32)
    within = slot_ids - page_start
    is_live = within < length
    return (doc_start + within, is_live)


def attn_kernel(
    first_ref, q_ref, g_hbm, qpos_ref, qseg_ref, kpos_ref, kseg_ref, o_ref, windows, sems,
    weight, weight_sem, attended, *, heads, scale, blocks, half, seq_count, kv_cols, weight_row,
    count,
):
    step = pl.program_id(0)
    weight_copy = pltpu.make_async_copy(
        g_hbm.at[pl.ds(weight_row, weight.shape[0])], weight, weight_sem.at[0]
    )

    def window_copies(slot):
        first = first_ref[slot]
        copies = []
        for k in range(blocks):
            block = first + k
            upper = block >= seq_count
            row = jnp.where(upper, half, 0)
            device = jnp.where(upper, 2 * seq_count - 1 - block, block)
            copies.append(
                pltpu.make_async_copy(
                    g_hbm.at[pl.ds(row, half), pl.ds(device * kv_cols, kv_cols)],
                    windows.at[slot, pl.ds(k * half, half)],
                    sems.at[slot, k],
                )
            )
        return copies

    pad = windows.shape[1] - blocks * half

    @pl.when(step == 0)
    def _():
        for slot in range(count):
            for copy in window_copies(slot):
                copy.start()
            if pad:
                windows[slot, pl.ds(blocks * half, pad), :] = jnp.zeros((pad, kv_cols), windows.dtype)
        weight_copy.start()

    for slot in range(count):

        @pl.when(step == slot)
        def _():
            for copy in window_copies(slot):
                copy.wait()

    window = windows.at[step]
    allowed = (kpos_ref[0] <= qpos_ref[0]) & (kseg_ref[0] == qseg_ref[0])
    key = window[:, :HD]
    value = window[:, HD:]
    for h in range(heads):
        query = q_ref[0, :, h * HD:(h + 1) * HD]
        scores = lax.dot_general(
            query, key, (((1,), (1,)), ((), ())), preferred_element_type=jnp.float32
        ) * scale
        scores = jnp.where(allowed, scores, -1e30)
        top = jnp.max(scores, axis=1, keepdims=True)
        weights = jnp.where(allowed, jnp.exp(scores - top), 0.0)
        total = jnp.sum(weights, axis=1, keepdims=True)
        summed = jnp.dot(weights.astype(jnp.bfloat16), value, preferred_element_type=jnp.float32)
        attended[:, h * HD:(h + 1) * HD] = (summed / total).astype(attended.dtype)

    @pl.when(step == 0)
    def _():
        weight_copy.wait()

    out_cols = o_ref.shape[2]
    chunk = 1024 if out_cols % 1024 == 0 else out_cols
    for c in range(out_cols // chunk):
        o_ref[0, :, c * chunk:(c + 1) * chunk] = jnp.dot(
            attended[...], weight[:, c * chunk:(c + 1) * chunk], preferred_element_type=jnp.float32
        ).astype(o_ref.dtype)


def attend(first, q, gathered, qpos, qseg, kpos, kseg, blocks, seq_count, kv_cols):
    count, rows, width = q.shape
    window_rows = kpos.shape[-1]
    heads = width // HD
    weight_row = count * rows
    out_cols = gathered.shape[1]
    kern = functools.partial(
        attn_kernel, heads=heads, scale=1.0 / math.sqrt(HD), blocks=blocks, half=rows,
        seq_count=seq_count, kv_cols=kv_cols, weight_row=weight_row, count=count,
    )
    grid_spec = pltpu.PrefetchScalarGridSpec(
        num_scalar_prefetch=1,
        grid=(count,),
        in_specs=[
            pl.BlockSpec((1, rows, width), lambda b, f: (b, 0, 0)),
            pl.BlockSpec(memory_space=pl.ANY),
            pl.BlockSpec((1, rows, 1), lambda b, f: (b, 0, 0)),
            pl.BlockSpec((1, rows, 1), lambda b, f: (b, 0, 0)),
            pl.BlockSpec((1, 1, window_rows), lambda b, f: (b, 0, 0)),
            pl.BlockSpec((1, 1, window_rows), lambda b, f: (b, 0, 0)),
        ],
        out_specs=pl.BlockSpec((1, rows, out_cols), lambda b, f: (b, 0, 0)),
        scratch_shapes=[
            pltpu.VMEM((count, window_rows, kv_cols), gathered.dtype),
            pltpu.SemaphoreType.DMA((count, blocks)),
            pltpu.VMEM((gathered.shape[0] - weight_row, out_cols), gathered.dtype),
            pltpu.SemaphoreType.DMA((1,)),
            pltpu.VMEM((rows, width), jnp.bfloat16),
        ],
    )
    return pl.pallas_call(
        kern,
        grid_spec=grid_spec,
        out_shape=jax.ShapeDtypeStruct((count, rows, out_cols), jnp.bfloat16),
        compiler_params=pltpu.CompilerParams(vmem_limit_bytes=56 * 1024 * 1024),
        cost_estimate=pl.CostEstimate(
            flops=4 * count * heads * rows * window_rows * HD + 2 * count * rows * width * out_cols,
            transcendentals=count * heads * rows * window_rows,
            bytes_accessed=count * (window_rows * kv_cols * 2 + rows * width * 2 + rows * out_cols * 2)
            + (gathered.shape[0] - weight_row) * out_cols * 2,
        ),
    )(first, q, gathered, qpos, qseg, kpos, kseg)


def norm_kernel(projected_ref, residual_ref, gain_ref, out_ref):
    hidden = residual_ref[...].astype(jnp.float32) + projected_ref[...].astype(jnp.float32)
    mean_square = jnp.mean(hidden * hidden, axis=-1, keepdims=True)
    out_ref[...] = (
        hidden * lax.rsqrt(mean_square + 1e-05) * gain_ref[...].astype(jnp.float32)
    ).astype(out_ref.dtype)


def residual_norm(projected, residual, gain, rows_per_step=80):
    rows, width = projected.shape
    steps = rows // rows_per_step
    return pl.pallas_call(
        norm_kernel,
        grid=(steps,),
        in_specs=[
            pl.BlockSpec((rows_per_step, width), lambda i: (i, 0)),
            pl.BlockSpec((rows_per_step, width), lambda i: (i, 0)),
            pl.BlockSpec((1, width), lambda i: (0, 0)),
        ],
        out_specs=pl.BlockSpec((rows_per_step, width), lambda i: (i, 0)),
        out_shape=jax.ShapeDtypeStruct((rows, width), jnp.bfloat16),
        cost_estimate=pl.CostEstimate(
            flops=5 * rows * width, transcendentals=rows, bytes_accessed=6 * rows * width
        ),
    )(projected, residual, gain.reshape(1, width))


def body(queries, key_rows, value_rows, out_weight, residual_in, norm_gain, prompt_lengths):
    seq_count = lax.axis_size("seq")
    seq_index = lax.axis_index("seq")
    per_device = queries.shape[0]
    half = per_device // 2
    kv_width = key_rows.shape[1]
    kv_rows = jnp.concatenate([key_rows, value_rows], axis=1)
    stacked = lax.all_gather(
        jnp.concatenate([kv_rows, out_weight], axis=0), "seq", axis=1, tiled=True
    )
    blocks = min(2 * seq_count, -(-(MAX_PROMPT - 1) // half) + 1)
    window = -(-(blocks * half) // 128) * 128
    block_index = jnp.stack([seq_index, 2 * seq_count - 1 - seq_index])
    first = jnp.clip(block_index - (blocks - 1), 0, 2 * seq_count - blocks).astype(jnp.int32)
    offsets = jnp.arange(window, dtype=jnp.int32)[None, :]
    key_position = jnp.where(
        offsets < blocks * half, first[:, None] * half + offsets, 4 * seq_count * per_device
    )
    query_position = block_index[:, None] * half + jnp.arange(half, dtype=jnp.int32)[None, :]
    key_segment = segment_of(key_position.reshape(-1), prompt_lengths).reshape(2, 1, window)
    query_segment = segment_of(query_position.reshape(-1), prompt_lengths).reshape(2, half, 1)
    partial_value = attend(
        first,
        queries.reshape(2, half, queries.shape[1]),
        stacked,
        query_position[:, :, None],
        query_segment,
        key_position[:, None, :],
        key_segment,
        blocks,
        seq_count,
        2 * kv_width,
    ).reshape(per_device, -1)
    partial_value, stacked = lax.optimization_barrier((partial_value, stacked))
    projected = lax.psum(partial_value, "tensor")
    normed = residual_norm(projected, residual_in, norm_gain)
    slot_ids = seq_index * SLOT_DEV + jnp.arange(SLOT_DEV, dtype=jnp.int32)
    source, is_live = slot_source(slot_ids, prompt_lengths, PAGE)
    target = stored_row(source, per_device, seq_count)
    empty_cache = jnp.zeros((SLOT_DEV, kv_width), jnp.bfloat16)
    kv_grid = stacked[:per_device].reshape(per_device, seq_count, 2 * kv_width)
    piece_rows = seq_count * per_device
    found = is_live & (target >= 0) & (target < piece_rows)
    safe_index = jnp.clip(target, 0, piece_rows - 1)
    cache_rows = kv_grid[safe_index % per_device, safe_index // per_device]
    cache_keys = jnp.where(found[:, None], cache_rows[:, :kv_width], empty_cache)
    cache_values = jnp.where(found[:, None], cache_rows[:, kv_width:], empty_cache)
    return (normed, cache_keys, cache_values)


def solution(mesh):
    return jax.shard_map(
        body,
        mesh=mesh,
        in_specs=(
            P("seq", "tensor"),
            P("seq", "tensor"),
            P("seq", "tensor"),
            P("tensor", "seq"),
            P("seq", None),
            P(),
            P(),
        ),
        out_specs=(P("seq", None), P("seq", "tensor"), P("seq", "tensor")),
        check_vma=False,
    )
```

```python
import functools
import math

import jax
import jax.numpy as jnp
from jax import lax
from jax.experimental import pallas as pl
from jax.experimental.pallas import tpu as pltpu
from jax.sharding import PartitionSpec as P

HD = 128
PAGE = 128
SLOT_DEV = 704
MAX_PROMPT = 5120


def position_of(stored, per_device, devices):
    half_block = per_device // 2
    device = stored // per_device
    offset = stored % per_device
    return jnp.where(
        offset < half_block,
        device * half_block + offset,
        (2 * devices - 1 - device) * half_block + offset - half_block,
    )


def stored_row(position, per_device, devices):
    half_block = per_device // 2
    block_index = position // half_block
    device = jnp.where(block_index < devices, block_index, 2 * devices - 1 - block_index)
    offset = position % half_block + jnp.where(block_index < devices, 0, half_block)
    return device * per_device + offset


def segment_of(position, lengths):
    doc_ends = jnp.cumsum(lengths, dtype=jnp.int32)
    return jnp.sum(
        (position[:, None] >= doc_ends[None, :]).astype(jnp.int32), axis=1, dtype=jnp.int32
    )


def slot_source(slot_ids, lengths, page_size):
    padded = (lengths + page_size - 1) // page_size * page_size
    page_ends = jnp.cumsum(padded, dtype=jnp.int32)
    page_starts = page_ends - padded
    doc_ends = jnp.cumsum(lengths, dtype=jnp.int32)
    doc_starts = doc_ends - lengths
    before = (slot_ids[:, None] >= page_ends[None, :]).astype(jnp.int32)
    inside = (slot_ids[:, None] >= page_starts[None, :]).astype(jnp.int32) - before
    page_start = jnp.sum(before * padded[None, :], axis=1, dtype=jnp.int32)
    doc_start = jnp.sum(before * lengths[None, :], axis=1, dtype=jnp.int32)
    length = jnp.sum(inside * lengths[None, :], axis=1, dtype=jnp.int32)
    within = slot_ids - page_start
    is_live = within < length
    return (doc_start + within, is_live)


def attn_kernel(
    first_ref, q_ref, g_hbm, qpos_ref, qseg_ref, kpos_ref, kseg_ref, o_ref, windows, sems,
    weight, weight_sem, attended, *, heads, scale, blocks, half, seq_count, kv_cols, weight_row,
    count,
):
    step = pl.program_id(0)
    weight_copy = pltpu.make_async_copy(
        g_hbm.at[pl.ds(weight_row, weight.shape[0])], weight, weight_sem.at[0]
    )

    def window_copies(slot):
        first = first_ref[slot]
        copies = []
        for k in range(blocks):
            block = first + k
            upper = block >= seq_count
            row = jnp.where(upper, half, 0)
            device = jnp.where(upper, 2 * seq_count - 1 - block, block)
            copies.append(
                pltpu.make_async_copy(
                    g_hbm.at[pl.ds(row, half), pl.ds(device * kv_cols, kv_cols)],
                    windows.at[slot, pl.ds(k * half, half)],
                    sems.at[slot, k],
                )
            )
        return copies

    pad = windows.shape[1] - blocks * half

    @pl.when(step == 0)
    def _():
        for slot in range(count):
            for copy in window_copies(slot):
                copy.start()
            if pad:
                windows[slot, pl.ds(blocks * half, pad), :] = jnp.zeros((pad, kv_cols), windows.dtype)
        weight_copy.start()

    for slot in range(count):

        @pl.when(step == slot)
        def _():
            for copy in window_copies(slot):
                copy.wait()

    window = windows.at[step]
    allowed = (kpos_ref[0] <= qpos_ref[0]) & (kseg_ref[0] == qseg_ref[0])
    key = window[:, :HD]
    value = window[:, HD:]
    for h in range(heads):
        query = q_ref[0, :, h * HD:(h + 1) * HD]
        scores = lax.dot_general(
            query, key, (((1,), (1,)), ((), ())), preferred_element_type=jnp.float32
        ) * scale
        scores = jnp.where(allowed, scores, -1e30)
        top = jnp.max(scores, axis=1, keepdims=True)
        weights = jnp.exp(scores - top)
        total = jnp.sum(weights, axis=1, keepdims=True)
        summed = jnp.dot(weights.astype(jnp.bfloat16), value, preferred_element_type=jnp.float32)
        attended[:, h * HD:(h + 1) * HD] = (summed / total).astype(attended.dtype)

    @pl.when(step == 0)
    def _():
        weight_copy.wait()

    out_cols = o_ref.shape[2]
    chunk = 1024 if out_cols % 1024 == 0 else out_cols
    for c in range(out_cols // chunk):
        o_ref[0, :, c * chunk:(c + 1) * chunk] = jnp.dot(
            attended[...], weight[:, c * chunk:(c + 1) * chunk], preferred_element_type=jnp.float32
        ).astype(o_ref.dtype)


def attend(first, q, gathered, qpos, qseg, kpos, kseg, blocks, seq_count, kv_cols):
    count, rows, width = q.shape
    window_rows = kpos.shape[-1]
    heads = width // HD
    weight_row = count * rows
    out_cols = gathered.shape[1]
    kern = functools.partial(
        attn_kernel, heads=heads, scale=1.0 / math.sqrt(HD), blocks=blocks, half=rows,
        seq_count=seq_count, kv_cols=kv_cols, weight_row=weight_row, count=count,
    )
    grid_spec = pltpu.PrefetchScalarGridSpec(
        num_scalar_prefetch=1,
        grid=(count,),
        in_specs=[
            pl.BlockSpec((1, rows, width), lambda b, f: (b, 0, 0)),
            pl.BlockSpec(memory_space=pl.ANY),
            pl.BlockSpec((1, rows, 1), lambda b, f: (b, 0, 0)),
            pl.BlockSpec((1, rows, 1), lambda b, f: (b, 0, 0)),
            pl.BlockSpec((1, 1, window_rows), lambda b, f: (b, 0, 0)),
            pl.BlockSpec((1, 1, window_rows), lambda b, f: (b, 0, 0)),
        ],
        out_specs=pl.BlockSpec((1, rows, out_cols), lambda b, f: (b, 0, 0)),
        scratch_shapes=[
            pltpu.VMEM((count, window_rows, kv_cols), gathered.dtype),
            pltpu.SemaphoreType.DMA((count, blocks)),
            pltpu.VMEM((gathered.shape[0] - weight_row, out_cols), gathered.dtype),
            pltpu.SemaphoreType.DMA((1,)),
            pltpu.VMEM((rows, width), jnp.bfloat16),
        ],
    )
    return pl.pallas_call(
        kern,
        grid_spec=grid_spec,
        out_shape=jax.ShapeDtypeStruct((count, rows, out_cols), jnp.bfloat16),
        compiler_params=pltpu.CompilerParams(vmem_limit_bytes=56 * 1024 * 1024),
        cost_estimate=pl.CostEstimate(
            flops=4 * count * heads * rows * window_rows * HD + 2 * count * rows * width * out_cols,
            transcendentals=count * heads * rows * window_rows,
            bytes_accessed=count * (window_rows * kv_cols * 2 + rows * width * 2 + rows * out_cols * 2)
            + (gathered.shape[0] - weight_row) * out_cols * 2,
        ),
    )(first, q, gathered, qpos, qseg, kpos, kseg)


def norm_kernel(projected_ref, residual_ref, gain_ref, out_ref):
    hidden = residual_ref[...].astype(jnp.float32) + projected_ref[...].astype(jnp.float32)
    mean_square = jnp.mean(hidden * hidden, axis=-1, keepdims=True)
    out_ref[...] = (
        hidden * lax.rsqrt(mean_square + 1e-05) * gain_ref[...].astype(jnp.float32)
    ).astype(out_ref.dtype)


def residual_norm(projected, residual, gain, rows_per_step=80):
    rows, width = projected.shape
    steps = rows // rows_per_step
    return pl.pallas_call(
        norm_kernel,
        grid=(steps,),
        in_specs=[
            pl.BlockSpec((rows_per_step, width), lambda i: (i, 0)),
            pl.BlockSpec((rows_per_step, width), lambda i: (i, 0)),
            pl.BlockSpec((1, width), lambda i: (0, 0)),
        ],
        out_specs=pl.BlockSpec((rows_per_step, width), lambda i: (i, 0)),
        out_shape=jax.ShapeDtypeStruct((rows, width), jnp.bfloat16),
        cost_estimate=pl.CostEstimate(
            flops=5 * rows * width, transcendentals=rows, bytes_accessed=6 * rows * width
        ),
    )(projected, residual, gain.reshape(1, width))


def body(queries, key_rows, value_rows, out_weight, residual_in, norm_gain, prompt_lengths):
    seq_count = lax.axis_size("seq")
    seq_index = lax.axis_index("seq")
    per_device = queries.shape[0]
    half = per_device // 2
    kv_width = key_rows.shape[1]
    kv_rows = jnp.concatenate([key_rows, value_rows], axis=1)
    stacked = lax.all_gather(
        jnp.concatenate([kv_rows, out_weight], axis=0), "seq", axis=1, tiled=True
    )
    blocks = min(2 * seq_count, -(-(MAX_PROMPT - 1) // half) + 1)
    window = -(-(blocks * half) // 128) * 128
    block_index = jnp.stack([seq_index, 2 * seq_count - 1 - seq_index])
    first = jnp.clip(block_index - (blocks - 1), 0, 2 * seq_count - blocks).astype(jnp.int32)
    offsets = jnp.arange(window, dtype=jnp.int32)[None, :]
    key_position = jnp.where(
        offsets < blocks * half, first[:, None] * half + offsets, 4 * seq_count * per_device
    )
    query_position = block_index[:, None] * half + jnp.arange(half, dtype=jnp.int32)[None, :]
    key_segment = segment_of(key_position.reshape(-1), prompt_lengths).reshape(2, 1, window)
    query_segment = segment_of(query_position.reshape(-1), prompt_lengths).reshape(2, half, 1)
    partial_value = attend(
        first,
        queries.reshape(2, half, queries.shape[1]),
        stacked,
        query_position[:, :, None],
        query_segment,
        key_position[:, None, :],
        key_segment,
        blocks,
        seq_count,
        2 * kv_width,
    ).reshape(per_device, -1)
    partial_value, stacked = lax.optimization_barrier((partial_value, stacked))
    projected = lax.psum(partial_value, "tensor")
    normed = residual_norm(projected, residual_in, norm_gain)
    slot_ids = seq_index * SLOT_DEV + jnp.arange(SLOT_DEV, dtype=jnp.int32)
    source, is_live = slot_source(slot_ids, prompt_lengths, PAGE)
    target = stored_row(source, per_device, seq_count)
    empty_cache = jnp.zeros((SLOT_DEV, kv_width), jnp.bfloat16)
    kv_grid = stacked[:per_device].reshape(per_device, seq_count, 2 * kv_width)
    piece_rows = seq_count * per_device
    found = is_live & (target >= 0) & (target < piece_rows)
    safe_index = jnp.clip(target, 0, piece_rows - 1)
    cache_rows = kv_grid[safe_index % per_device, safe_index // per_device]
    cache_keys = jnp.where(found[:, None], cache_rows[:, :kv_width], empty_cache)
    cache_values = jnp.where(found[:, None], cache_rows[:, kv_width:], empty_cache)
    return (normed, cache_keys, cache_values)


def solution(mesh):
    return jax.shard_map(
        body,
        mesh=mesh,
        in_specs=(
            P("seq", "tensor"),
            P("seq", "tensor"),
            P("seq", "tensor"),
            P("tensor", "seq"),
            P("seq", None),
            P(),
            P(),
        ),
        out_specs=(P("seq", None), P("seq", "tensor"), P("seq", "tensor")),
        check_vma=False,
    )
```

```python
import functools
import math

import jax
import jax.numpy as jnp
from jax import lax
from jax.experimental import pallas as pl
from jax.experimental.pallas import tpu as pltpu
from jax.sharding import PartitionSpec as P

HD = 128
PAGE = 128
SLOT_DEV = 704
MAX_PROMPT = 5120


def position_of(stored, per_device, devices):
    half_block = per_device // 2
    device = stored // per_device
    offset = stored % per_device
    return jnp.where(
        offset < half_block,
        device * half_block + offset,
        (2 * devices - 1 - device) * half_block + offset - half_block,
    )


def stored_row(position, per_device, devices):
    half_block = per_device // 2
    block_index = position // half_block
    device = jnp.where(block_index < devices, block_index, 2 * devices - 1 - block_index)
    offset = position % half_block + jnp.where(block_index < devices, 0, half_block)
    return device * per_device + offset


def segment_of(position, lengths):
    doc_ends = jnp.cumsum(lengths, dtype=jnp.int32)
    return jnp.sum(
        (position[:, None] >= doc_ends[None, :]).astype(jnp.int32), axis=1, dtype=jnp.int32
    )


def slot_source(slot_ids, lengths, page_size):
    padded = (lengths + page_size - 1) // page_size * page_size
    page_ends = jnp.cumsum(padded, dtype=jnp.int32)
    page_starts = page_ends - padded
    doc_ends = jnp.cumsum(lengths, dtype=jnp.int32)
    doc_starts = doc_ends - lengths
    before = (slot_ids[:, None] >= page_ends[None, :]).astype(jnp.int32)
    inside = (slot_ids[:, None] >= page_starts[None, :]).astype(jnp.int32) - before
    page_start = jnp.sum(before * padded[None, :], axis=1, dtype=jnp.int32)
    doc_start = jnp.sum(before * lengths[None, :], axis=1, dtype=jnp.int32)
    length = jnp.sum(inside * lengths[None, :], axis=1, dtype=jnp.int32)
    within = slot_ids - page_start
    is_live = within < length
    return (doc_start + within, is_live)


def attn_kernel(
    first_ref, q_ref, g_hbm, qpos_ref, qseg_ref, kpos_ref, kseg_ref, o_ref, windows, sems,
    weight, weight_sem, attended, *, heads, scale, blocks, half, seq_count, kv_cols, weight_row,
    count,
):
    step = pl.program_id(0)
    weight_copy = pltpu.make_async_copy(
        g_hbm.at[pl.ds(weight_row, weight.shape[0])], weight, weight_sem.at[0]
    )

    def window_copies(slot):
        first = first_ref[slot]
        copies = []
        for k in range(blocks):
            block = first + k
            upper = block >= seq_count
            row = jnp.where(upper, half, 0)
            device = jnp.where(upper, 2 * seq_count - 1 - block, block)
            copies.append(
                pltpu.make_async_copy(
                    g_hbm.at[pl.ds(row, half), pl.ds(device * kv_cols, kv_cols)],
                    windows.at[slot, pl.ds(k * half, half)],
                    sems.at[slot, k],
                )
            )
        return copies

    pad = windows.shape[1] - blocks * half

    @pl.when(step == 0)
    def _():
        for slot in range(count):
            for copy in window_copies(slot):
                copy.start()
            if pad:
                windows[slot, pl.ds(blocks * half, pad), :] = jnp.zeros((pad, kv_cols), windows.dtype)
        weight_copy.start()

    for slot in range(count):

        @pl.when(step == slot)
        def _():
            for copy in window_copies(slot):
                copy.wait()

    window = windows.at[step]
    allowed = (kpos_ref[0] <= qpos_ref[0]) & (kseg_ref[0] == qseg_ref[0])
    key = window[:, :HD]
    value = window[:, HD:]
    for h in range(heads):
        query = q_ref[0, :, h * HD:(h + 1) * HD]
        scores = lax.dot_general(
            query, key, (((1,), (1,)), ((), ())), preferred_element_type=jnp.float32
        ) * scale
        scores = jnp.where(allowed, scores, -1e30)
        top = jnp.max(scores, axis=1, keepdims=True)
        weights = jnp.exp(scores - top)
        total = jnp.sum(weights, axis=1, keepdims=True)
        summed = jnp.dot(weights.astype(jnp.bfloat16), value, preferred_element_type=jnp.float32)
        attended[:, h * HD:(h + 1) * HD] = (summed / total).astype(attended.dtype)

    @pl.when(step == 0)
    def _():
        weight_copy.wait()

    out_cols = o_ref.shape[2]
    chunk = 1024 if out_cols % 1024 == 0 else out_cols
    for c in range(out_cols // chunk):
        o_ref[0, :, c * chunk:(c + 1) * chunk] = jnp.dot(
            attended[...], weight[:, c * chunk:(c + 1) * chunk], preferred_element_type=jnp.float32
        ).astype(o_ref.dtype)


def attend(first, q, gathered, qpos, qseg, kpos, kseg, blocks, seq_count, kv_cols):
    count, rows, width = q.shape
    window_rows = kpos.shape[-1]
    heads = width // HD
    weight_row = count * rows
    out_cols = gathered.shape[1]
    kern = functools.partial(
        attn_kernel, heads=heads, scale=1.0 / math.sqrt(HD), blocks=blocks, half=rows,
        seq_count=seq_count, kv_cols=kv_cols, weight_row=weight_row, count=count,
    )
    grid_spec = pltpu.PrefetchScalarGridSpec(
        num_scalar_prefetch=1,
        grid=(count,),
        in_specs=[
            pl.BlockSpec((1, rows, width), lambda b, f: (b, 0, 0)),
            pl.BlockSpec(memory_space=pl.ANY),
            pl.BlockSpec((1, rows, 1), lambda b, f: (b, 0, 0)),
            pl.BlockSpec((1, rows, 1), lambda b, f: (b, 0, 0)),
            pl.BlockSpec((1, 1, window_rows), lambda b, f: (b, 0, 0)),
            pl.BlockSpec((1, 1, window_rows), lambda b, f: (b, 0, 0)),
        ],
        out_specs=pl.BlockSpec((1, rows, out_cols), lambda b, f: (b, 0, 0)),
        scratch_shapes=[
            pltpu.VMEM((count, window_rows, kv_cols), gathered.dtype),
            pltpu.SemaphoreType.DMA((count, blocks)),
            pltpu.VMEM((gathered.shape[0] - weight_row, out_cols), gathered.dtype),
            pltpu.SemaphoreType.DMA((1,)),
            pltpu.VMEM((rows, width), jnp.bfloat16),
        ],
    )
    return pl.pallas_call(
        kern,
        grid_spec=grid_spec,
        out_shape=jax.ShapeDtypeStruct((count, rows, out_cols), jnp.bfloat16),
        compiler_params=pltpu.CompilerParams(vmem_limit_bytes=56 * 1024 * 1024),
        cost_estimate=pl.CostEstimate(
            flops=4 * count * heads * rows * window_rows * HD + 2 * count * rows * width * out_cols,
            transcendentals=count * heads * rows * window_rows,
            bytes_accessed=count * (window_rows * kv_cols * 2 + rows * width * 2 + rows * out_cols * 2)
            + (gathered.shape[0] - weight_row) * out_cols * 2,
        ),
    )(first, q, gathered, qpos, qseg, kpos, kseg)


def norm_kernel(projected_ref, residual_ref, gain_ref, out_ref):
    hidden = residual_ref[...].astype(jnp.float32) + projected_ref[...].astype(jnp.float32)
    mean_square = jnp.mean(hidden * hidden, axis=-1, keepdims=True)
    out_ref[...] = (
        hidden * lax.rsqrt(mean_square + 1e-05) * gain_ref[...].astype(jnp.float32)
    ).astype(out_ref.dtype)


def residual_norm(projected, residual, gain, rows_per_step=160):
    rows, width = projected.shape
    steps = rows // rows_per_step
    return pl.pallas_call(
        norm_kernel,
        grid=(steps,),
        in_specs=[
            pl.BlockSpec((rows_per_step, width), lambda i: (i, 0)),
            pl.BlockSpec((rows_per_step, width), lambda i: (i, 0)),
            pl.BlockSpec((1, width), lambda i: (0, 0)),
        ],
        out_specs=pl.BlockSpec((rows_per_step, width), lambda i: (i, 0)),
        out_shape=jax.ShapeDtypeStruct((rows, width), jnp.bfloat16),
        cost_estimate=pl.CostEstimate(
            flops=5 * rows * width, transcendentals=rows, bytes_accessed=6 * rows * width
        ),
    )(projected, residual, gain.reshape(1, width))


def body(queries, key_rows, value_rows, out_weight, residual_in, norm_gain, prompt_lengths):
    seq_count = lax.axis_size("seq")
    seq_index = lax.axis_index("seq")
    per_device = queries.shape[0]
    half = per_device // 2
    kv_width = key_rows.shape[1]
    kv_rows = jnp.concatenate([key_rows, value_rows], axis=1)
    stacked = lax.all_gather(
        jnp.concatenate([kv_rows, out_weight], axis=0), "seq", axis=1, tiled=True
    )
    blocks = min(2 * seq_count, -(-(MAX_PROMPT - 1) // half) + 1)
    window = -(-(blocks * half) // 128) * 128
    block_index = jnp.stack([seq_index, 2 * seq_count - 1 - seq_index])
    first = jnp.clip(block_index - (blocks - 1), 0, 2 * seq_count - blocks).astype(jnp.int32)
    offsets = jnp.arange(window, dtype=jnp.int32)[None, :]
    key_position = jnp.where(
        offsets < blocks * half, first[:, None] * half + offsets, 4 * seq_count * per_device
    )
    query_position = block_index[:, None] * half + jnp.arange(half, dtype=jnp.int32)[None, :]
    key_segment = segment_of(key_position.reshape(-1), prompt_lengths).reshape(2, 1, window)
    query_segment = segment_of(query_position.reshape(-1), prompt_lengths).reshape(2, half, 1)
    partial_value = attend(
        first,
        queries.reshape(2, half, queries.shape[1]),
        stacked,
        query_position[:, :, None],
        query_segment,
        key_position[:, None, :],
        key_segment,
        blocks,
        seq_count,
        2 * kv_width,
    ).reshape(per_device, -1)
    partial_value, stacked = lax.optimization_barrier((partial_value, stacked))
    projected = lax.psum(partial_value, "tensor")
    normed = residual_norm(projected, residual_in, norm_gain)
    slot_ids = seq_index * SLOT_DEV + jnp.arange(SLOT_DEV, dtype=jnp.int32)
    source, is_live = slot_source(slot_ids, prompt_lengths, PAGE)
    target = stored_row(source, per_device, seq_count)
    empty_cache = jnp.zeros((SLOT_DEV, kv_width), jnp.bfloat16)
    kv_grid = stacked[:per_device].reshape(per_device, seq_count, 2 * kv_width)
    piece_rows = seq_count * per_device
    found = is_live & (target >= 0) & (target < piece_rows)
    safe_index = jnp.clip(target, 0, piece_rows - 1)
    cache_rows = kv_grid[safe_index % per_device, safe_index // per_device]
    cache_keys = jnp.where(found[:, None], cache_rows[:, :kv_width], empty_cache)
    cache_values = jnp.where(found[:, None], cache_rows[:, kv_width:], empty_cache)
    return (normed, cache_keys, cache_values)


def solution(mesh):
    return jax.shard_map(
        body,
        mesh=mesh,
        in_specs=(
            P("seq", "tensor"),
            P("seq", "tensor"),
            P("seq", "tensor"),
            P("tensor", "seq"),
            P("seq", None),
            P(),
            P(),
        ),
        out_specs=(P("seq", None), P("seq", "tensor"), P("seq", "tensor")),
        check_vma=False,
    )
```

```python
import functools
import math

import jax
import jax.numpy as jnp
from jax import lax
from jax.experimental import pallas as pl
from jax.experimental.pallas import tpu as pltpu
from jax.sharding import PartitionSpec as P

HD = 128
PAGE = 128
SLOT_DEV = 704
MAX_PROMPT = 5120


def position_of(stored, per_device, devices):
    half_block = per_device // 2
    device = stored // per_device
    offset = stored % per_device
    return jnp.where(
        offset < half_block,
        device * half_block + offset,
        (2 * devices - 1 - device) * half_block + offset - half_block,
    )


def stored_row(position, per_device, devices):
    half_block = per_device // 2
    block_index = position // half_block
    device = jnp.where(block_index < devices, block_index, 2 * devices - 1 - block_index)
    offset = position % half_block + jnp.where(block_index < devices, 0, half_block)
    return device * per_device + offset


def segment_of(position, lengths):
    doc_ends = jnp.cumsum(lengths, dtype=jnp.int32)
    return jnp.sum(
        (position[:, None] >= doc_ends[None, :]).astype(jnp.int32), axis=1, dtype=jnp.int32
    )


def slot_source(slot_ids, lengths, page_size):
    padded = (lengths + page_size - 1) // page_size * page_size
    page_ends = jnp.cumsum(padded, dtype=jnp.int32)
    page_starts = page_ends - padded
    doc_ends = jnp.cumsum(lengths, dtype=jnp.int32)
    doc_starts = doc_ends - lengths
    before = (slot_ids[:, None] >= page_ends[None, :]).astype(jnp.int32)
    inside = (slot_ids[:, None] >= page_starts[None, :]).astype(jnp.int32) - before
    page_start = jnp.sum(before * padded[None, :], axis=1, dtype=jnp.int32)
    doc_start = jnp.sum(before * lengths[None, :], axis=1, dtype=jnp.int32)
    length = jnp.sum(inside * lengths[None, :], axis=1, dtype=jnp.int32)
    within = slot_ids - page_start
    is_live = within < length
    return (doc_start + within, is_live)


def attn_kernel(
    first_ref, q_ref, g_hbm, qpos_ref, qseg_ref, kpos_ref, kseg_ref, o_ref, windows, sems,
    weight, weight_sem, attended, *, heads, scale, blocks, half, seq_count, kv_cols, weight_row,
    count,
):
    step = pl.program_id(0)
    weight_copy = pltpu.make_async_copy(
        g_hbm.at[pl.ds(weight_row, weight.shape[0])], weight, weight_sem.at[0]
    )

    def window_copies(slot):
        first = first_ref[slot]
        copies = []
        for k in range(blocks):
            block = first + k
            upper = block >= seq_count
            row = jnp.where(upper, half, 0)
            device = jnp.where(upper, 2 * seq_count - 1 - block, block)
            copies.append(
                pltpu.make_async_copy(
                    g_hbm.at[pl.ds(row, half), pl.ds(device * kv_cols, kv_cols)],
                    windows.at[slot, pl.ds(k * half, half)],
                    sems.at[slot, k],
                )
            )
        return copies

    pad = windows.shape[1] - blocks * half

    @pl.when(step == 0)
    def _():
        for slot in range(count):
            for copy in window_copies(slot):
                copy.start()
            if pad:
                windows[slot, pl.ds(blocks * half, pad), :] = jnp.zeros((pad, kv_cols), windows.dtype)
        weight_copy.start()

    for slot in range(count):

        @pl.when(step == slot)
        def _():
            for copy in window_copies(slot):
                copy.wait()

    window = windows.at[step]
    allowed = (kpos_ref[0] <= qpos_ref[0]) & (kseg_ref[0] == qseg_ref[0])
    key = window[:, :HD]
    value = window[:, HD:]
    for h in range(heads):
        query = q_ref[0, :, h * HD:(h + 1) * HD]
        scores = lax.dot_general(
            query, key, (((1,), (1,)), ((), ())), preferred_element_type=jnp.float32
        ) * scale
        scores = jnp.where(allowed, scores, -1e30)
        top = jnp.max(scores, axis=1, keepdims=True)
        weights = jnp.exp(scores - top)
        total = jnp.sum(weights, axis=1, keepdims=True)
        summed = jnp.dot(weights.astype(jnp.bfloat16), value, preferred_element_type=jnp.float32)
        attended[:, h * HD:(h + 1) * HD] = (summed / total).astype(attended.dtype)

    @pl.when(step == 0)
    def _():
        weight_copy.wait()

    out_cols = o_ref.shape[2]
    chunk = 2048 if out_cols % 2048 == 0 else out_cols
    for c in range(out_cols // chunk):
        o_ref[0, :, c * chunk:(c + 1) * chunk] = jnp.dot(
            attended[...], weight[:, c * chunk:(c + 1) * chunk], preferred_element_type=jnp.float32
        ).astype(o_ref.dtype)


def attend(first, q, gathered, qpos, qseg, kpos, kseg, blocks, seq_count, kv_cols):
    count, rows, width = q.shape
    window_rows = kpos.shape[-1]
    heads = width // HD
    weight_row = count * rows
    out_cols = gathered.shape[1]
    kern = functools.partial(
        attn_kernel, heads=heads, scale=1.0 / math.sqrt(HD), blocks=blocks, half=rows,
        seq_count=seq_count, kv_cols=kv_cols, weight_row=weight_row, count=count,
    )
    grid_spec = pltpu.PrefetchScalarGridSpec(
        num_scalar_prefetch=1,
        grid=(count,),
        in_specs=[
            pl.BlockSpec((1, rows, width), lambda b, f: (b, 0, 0)),
            pl.BlockSpec(memory_space=pl.ANY),
            pl.BlockSpec((1, rows, 1), lambda b, f: (b, 0, 0)),
            pl.BlockSpec((1, rows, 1), lambda b, f: (b, 0, 0)),
            pl.BlockSpec((1, 1, window_rows), lambda b, f: (b, 0, 0)),
            pl.BlockSpec((1, 1, window_rows), lambda b, f: (b, 0, 0)),
        ],
        out_specs=pl.BlockSpec((1, rows, out_cols), lambda b, f: (b, 0, 0)),
        scratch_shapes=[
            pltpu.VMEM((count, window_rows, kv_cols), gathered.dtype),
            pltpu.SemaphoreType.DMA((count, blocks)),
            pltpu.VMEM((gathered.shape[0] - weight_row, out_cols), gathered.dtype),
            pltpu.SemaphoreType.DMA((1,)),
            pltpu.VMEM((rows, width), jnp.bfloat16),
        ],
    )
    return pl.pallas_call(
        kern,
        grid_spec=grid_spec,
        out_shape=jax.ShapeDtypeStruct((count, rows, out_cols), jnp.bfloat16),
        compiler_params=pltpu.CompilerParams(vmem_limit_bytes=56 * 1024 * 1024),
        cost_estimate=pl.CostEstimate(
            flops=4 * count * heads * rows * window_rows * HD + 2 * count * rows * width * out_cols,
            transcendentals=count * heads * rows * window_rows,
            bytes_accessed=count * (window_rows * kv_cols * 2 + rows * width * 2 + rows * out_cols * 2)
            + (gathered.shape[0] - weight_row) * out_cols * 2,
        ),
    )(first, q, gathered, qpos, qseg, kpos, kseg)


def norm_kernel(projected_ref, residual_ref, gain_ref, out_ref):
    hidden = residual_ref[...].astype(jnp.float32) + projected_ref[...].astype(jnp.float32)
    mean_square = jnp.mean(hidden * hidden, axis=-1, keepdims=True)
    out_ref[...] = (
        hidden * lax.rsqrt(mean_square + 1e-05) * gain_ref[...].astype(jnp.float32)
    ).astype(out_ref.dtype)


def residual_norm(projected, residual, gain, rows_per_step=80):
    rows, width = projected.shape
    steps = rows // rows_per_step
    return pl.pallas_call(
        norm_kernel,
        grid=(steps,),
        in_specs=[
            pl.BlockSpec((rows_per_step, width), lambda i: (i, 0)),
            pl.BlockSpec((rows_per_step, width), lambda i: (i, 0)),
            pl.BlockSpec((1, width), lambda i: (0, 0)),
        ],
        out_specs=pl.BlockSpec((rows_per_step, width), lambda i: (i, 0)),
        out_shape=jax.ShapeDtypeStruct((rows, width), jnp.bfloat16),
        cost_estimate=pl.CostEstimate(
            flops=5 * rows * width, transcendentals=rows, bytes_accessed=6 * rows * width
        ),
    )(projected, residual, gain.reshape(1, width))


def body(queries, key_rows, value_rows, out_weight, residual_in, norm_gain, prompt_lengths):
    seq_count = lax.axis_size("seq")
    seq_index = lax.axis_index("seq")
    per_device = queries.shape[0]
    half = per_device // 2
    kv_width = key_rows.shape[1]
    kv_rows = jnp.concatenate([key_rows, value_rows], axis=1)
    stacked = lax.all_gather(
        jnp.concatenate([kv_rows, out_weight], axis=0), "seq", axis=1, tiled=True
    )
    blocks = min(2 * seq_count, -(-(MAX_PROMPT - 1) // half) + 1)
    window = -(-(blocks * half) // 128) * 128
    block_index = jnp.stack([seq_index, 2 * seq_count - 1 - seq_index])
    first = jnp.clip(block_index - (blocks - 1), 0, 2 * seq_count - blocks).astype(jnp.int32)
    offsets = jnp.arange(window, dtype=jnp.int32)[None, :]
    key_position = jnp.where(
        offsets < blocks * half, first[:, None] * half + offsets, 4 * seq_count * per_device
    )
    query_position = block_index[:, None] * half + jnp.arange(half, dtype=jnp.int32)[None, :]
    key_segment = segment_of(key_position.reshape(-1), prompt_lengths).reshape(2, 1, window)
    query_segment = segment_of(query_position.reshape(-1), prompt_lengths).reshape(2, half, 1)
    partial_value = attend(
        first,
        queries.reshape(2, half, queries.shape[1]),
        stacked,
        query_position[:, :, None],
        query_segment,
        key_position[:, None, :],
        key_segment,
        blocks,
        seq_count,
        2 * kv_width,
    ).reshape(per_device, -1)
    partial_value, stacked = lax.optimization_barrier((partial_value, stacked))
    projected = lax.psum(partial_value, "tensor")
    normed = residual_norm(projected, residual_in, norm_gain)
    slot_ids = seq_index * SLOT_DEV + jnp.arange(SLOT_DEV, dtype=jnp.int32)
    source, is_live = slot_source(slot_ids, prompt_lengths, PAGE)
    target = stored_row(source, per_device, seq_count)
    empty_cache = jnp.zeros((SLOT_DEV, kv_width), jnp.bfloat16)
    kv_grid = stacked[:per_device].reshape(per_device, seq_count, 2 * kv_width)
    piece_rows = seq_count * per_device
    found = is_live & (target >= 0) & (target < piece_rows)
    safe_index = jnp.clip(target, 0, piece_rows - 1)
    cache_rows = kv_grid[safe_index % per_device, safe_index // per_device]
    cache_keys = jnp.where(found[:, None], cache_rows[:, :kv_width], empty_cache)
    cache_values = jnp.where(found[:, None], cache_rows[:, kv_width:], empty_cache)
    return (normed, cache_keys, cache_values)


def solution(mesh):
    return jax.shard_map(
        body,
        mesh=mesh,
        in_specs=(
            P("seq", "tensor"),
            P("seq", "tensor"),
            P("seq", "tensor"),
            P("tensor", "seq"),
            P("seq", None),
            P(),
            P(),
        ),
        out_specs=(P("seq", None), P("seq", "tensor"), P("seq", "tensor")),
        check_vma=False,
    )
```

```python
import functools
import math

import jax
import jax.numpy as jnp
from jax import lax
from jax.experimental import pallas as pl
from jax.experimental.pallas import tpu as pltpu
from jax.sharding import PartitionSpec as P

HD = 128
PAGE = 128
SLOT_DEV = 704
MAX_PROMPT = 5120


def position_of(stored, per_device, devices):
    half_block = per_device // 2
    device = stored // per_device
    offset = stored % per_device
    return jnp.where(
        offset < half_block,
        device * half_block + offset,
        (2 * devices - 1 - device) * half_block + offset - half_block,
    )


def stored_row(position, per_device, devices):
    half_block = per_device // 2
    block_index = position // half_block
    device = jnp.where(block_index < devices, block_index, 2 * devices - 1 - block_index)
    offset = position % half_block + jnp.where(block_index < devices, 0, half_block)
    return device * per_device + offset


def segment_of(position, lengths):
    doc_ends = jnp.cumsum(lengths, dtype=jnp.int32)
    return jnp.sum(
        (position[:, None] >= doc_ends[None, :]).astype(jnp.int32), axis=1, dtype=jnp.int32
    )


def slot_source(slot_ids, lengths, page_size):
    padded = (lengths + page_size - 1) // page_size * page_size
    page_ends = jnp.cumsum(padded, dtype=jnp.int32)
    page_starts = page_ends - padded
    doc_ends = jnp.cumsum(lengths, dtype=jnp.int32)
    doc_starts = doc_ends - lengths
    before = (slot_ids[:, None] >= page_ends[None, :]).astype(jnp.int32)
    inside = (slot_ids[:, None] >= page_starts[None, :]).astype(jnp.int32) - before
    page_start = jnp.sum(before * padded[None, :], axis=1, dtype=jnp.int32)
    doc_start = jnp.sum(before * lengths[None, :], axis=1, dtype=jnp.int32)
    length = jnp.sum(inside * lengths[None, :], axis=1, dtype=jnp.int32)
    within = slot_ids - page_start
    is_live = within < length
    return (doc_start + within, is_live)


def attn_kernel(
    first_ref, q_ref, g_hbm, qpos_ref, qseg_ref, kpos_ref, kseg_ref, o_ref, windows, sems,
    weight, weight_sem, attended, *, heads, scale, blocks, half, seq_count, kv_cols, weight_row,
    count,
):
    step = pl.program_id(0)
    weight_copy = pltpu.make_async_copy(
        g_hbm.at[pl.ds(weight_row, weight.shape[0])], weight, weight_sem.at[0]
    )

    def window_copies(slot):
        first = first_ref[slot]
        copies = []
        for k in range(blocks):
            block = first + k
            upper = block >= seq_count
            row = jnp.where(upper, half, 0)
            device = jnp.where(upper, 2 * seq_count - 1 - block, block)
            copies.append(
                pltpu.make_async_copy(
                    g_hbm.at[pl.ds(row, half), pl.ds(device * kv_cols, kv_cols)],
                    windows.at[slot, pl.ds(k * half, half)],
                    sems.at[slot, k],
                )
            )
        return copies

    pad = windows.shape[1] - blocks * half

    @pl.when(step == 0)
    def _():
        for slot in range(count):
            for copy in window_copies(slot):
                copy.start()
            if pad:
                windows[slot, pl.ds(blocks * half, pad), :] = jnp.zeros((pad, kv_cols), windows.dtype)
        weight_copy.start()

    for slot in range(count):

        @pl.when(step == slot)
        def _():
            for copy in window_copies(slot):
                copy.wait()

    window = windows.at[step]
    pair = 2 if heads % 2 == 0 else 1
    rows = q_ref.shape[1]
    query_position = jnp.concatenate([qpos_ref[0]] * pair, axis=0)
    query_segment = jnp.concatenate([qseg_ref[0]] * pair, axis=0)
    allowed = (kpos_ref[0] <= query_position) & (kseg_ref[0] == query_segment)
    key = window[:, :HD]
    value = window[:, HD:]
    for g in range(heads // pair):
        query = jnp.concatenate(
            [q_ref[0, :, (g * pair + p) * HD:(g * pair + p + 1) * HD] for p in range(pair)], axis=0
        )
        scores = lax.dot_general(
            query, key, (((1,), (1,)), ((), ())), preferred_element_type=jnp.float32
        ) * scale
        scores = jnp.where(allowed, scores, -1e30)
        top = jnp.max(scores, axis=1, keepdims=True)
        weights = jnp.exp(scores - top)
        total = jnp.sum(weights, axis=1, keepdims=True)
        summed = jnp.dot(weights.astype(jnp.bfloat16), value, preferred_element_type=jnp.float32)
        result = (summed / total).astype(attended.dtype)
        for p in range(pair):
            h = g * pair + p
            attended[:, h * HD:(h + 1) * HD] = result[p * rows:(p + 1) * rows]

    @pl.when(step == 0)
    def _():
        weight_copy.wait()

    out_cols = o_ref.shape[2]
    chunk = 1024 if out_cols % 1024 == 0 else out_cols
    for c in range(out_cols // chunk):
        o_ref[0, :, c * chunk:(c + 1) * chunk] = jnp.dot(
            attended[...], weight[:, c * chunk:(c + 1) * chunk], preferred_element_type=jnp.float32
        ).astype(o_ref.dtype)


def attend(first, q, gathered, qpos, qseg, kpos, kseg, blocks, seq_count, kv_cols):
    count, rows, width = q.shape
    window_rows = kpos.shape[-1]
    heads = width // HD
    weight_row = count * rows
    out_cols = gathered.shape[1]
    kern = functools.partial(
        attn_kernel, heads=heads, scale=1.0 / math.sqrt(HD), blocks=blocks, half=rows,
        seq_count=seq_count, kv_cols=kv_cols, weight_row=weight_row, count=count,
    )
    grid_spec = pltpu.PrefetchScalarGridSpec(
        num_scalar_prefetch=1,
        grid=(count,),
        in_specs=[
            pl.BlockSpec((1, rows, width), lambda b, f: (b, 0, 0)),
            pl.BlockSpec(memory_space=pl.ANY),
            pl.BlockSpec((1, rows, 1), lambda b, f: (b, 0, 0)),
            pl.BlockSpec((1, rows, 1), lambda b, f: (b, 0, 0)),
            pl.BlockSpec((1, 1, window_rows), lambda b, f: (b, 0, 0)),
            pl.BlockSpec((1, 1, window_rows), lambda b, f: (b, 0, 0)),
        ],
        out_specs=pl.BlockSpec((1, rows, out_cols), lambda b, f: (b, 0, 0)),
        scratch_shapes=[
            pltpu.VMEM((count, window_rows, kv_cols), gathered.dtype),
            pltpu.SemaphoreType.DMA((count, blocks)),
            pltpu.VMEM((gathered.shape[0] - weight_row, out_cols), gathered.dtype),
            pltpu.SemaphoreType.DMA((1,)),
            pltpu.VMEM((rows, width), jnp.bfloat16),
        ],
    )
    return pl.pallas_call(
        kern,
        grid_spec=grid_spec,
        out_shape=jax.ShapeDtypeStruct((count, rows, out_cols), jnp.bfloat16),
        compiler_params=pltpu.CompilerParams(vmem_limit_bytes=56 * 1024 * 1024),
        cost_estimate=pl.CostEstimate(
            flops=4 * count * heads * rows * window_rows * HD + 2 * count * rows * width * out_cols,
            transcendentals=count * heads * rows * window_rows,
            bytes_accessed=count * (window_rows * kv_cols * 2 + rows * width * 2 + rows * out_cols * 2)
            + (gathered.shape[0] - weight_row) * out_cols * 2,
        ),
    )(first, q, gathered, qpos, qseg, kpos, kseg)


def norm_kernel(projected_ref, residual_ref, gain_ref, out_ref):
    hidden = residual_ref[...].astype(jnp.float32) + projected_ref[...].astype(jnp.float32)
    mean_square = jnp.mean(hidden * hidden, axis=-1, keepdims=True)
    out_ref[...] = (
        hidden * lax.rsqrt(mean_square + 1e-05) * gain_ref[...].astype(jnp.float32)
    ).astype(out_ref.dtype)


def residual_norm(projected, residual, gain, rows_per_step=80):
    rows, width = projected.shape
    steps = rows // rows_per_step
    return pl.pallas_call(
        norm_kernel,
        grid=(steps,),
        in_specs=[
            pl.BlockSpec((rows_per_step, width), lambda i: (i, 0)),
            pl.BlockSpec((rows_per_step, width), lambda i: (i, 0)),
            pl.BlockSpec((1, width), lambda i: (0, 0)),
        ],
        out_specs=pl.BlockSpec((rows_per_step, width), lambda i: (i, 0)),
        out_shape=jax.ShapeDtypeStruct((rows, width), jnp.bfloat16),
        cost_estimate=pl.CostEstimate(
            flops=5 * rows * width, transcendentals=rows, bytes_accessed=6 * rows * width
        ),
    )(projected, residual, gain.reshape(1, width))


def body(queries, key_rows, value_rows, out_weight, residual_in, norm_gain, prompt_lengths):
    seq_count = lax.axis_size("seq")
    seq_index = lax.axis_index("seq")
    per_device = queries.shape[0]
    half = per_device // 2
    kv_width = key_rows.shape[1]
    kv_rows = jnp.concatenate([key_rows, value_rows], axis=1)
    stacked = lax.all_gather(
        jnp.concatenate([kv_rows, out_weight], axis=0), "seq", axis=1, tiled=True
    )
    blocks = min(2 * seq_count, -(-(MAX_PROMPT - 1) // half) + 1)
    window = -(-(blocks * half) // 128) * 128
    block_index = jnp.stack([seq_index, 2 * seq_count - 1 - seq_index])
    first = jnp.clip(block_index - (blocks - 1), 0, 2 * seq_count - blocks).astype(jnp.int32)
    offsets = jnp.arange(window, dtype=jnp.int32)[None, :]
    key_position = jnp.where(
        offsets < blocks * half, first[:, None] * half + offsets, 4 * seq_count * per_device
    )
    query_position = block_index[:, None] * half + jnp.arange(half, dtype=jnp.int32)[None, :]
    key_segment = segment_of(key_position.reshape(-1), prompt_lengths).reshape(2, 1, window)
    query_segment = segment_of(query_position.reshape(-1), prompt_lengths).reshape(2, half, 1)
    partial_value = attend(
        first,
        queries.reshape(2, half, queries.shape[1]),
        stacked,
        query_position[:, :, None],
        query_segment,
        key_position[:, None, :],
        key_segment,
        blocks,
        seq_count,
        2 * kv_width,
    ).reshape(per_device, -1)
    partial_value, stacked = lax.optimization_barrier((partial_value, stacked))
    projected = lax.psum(partial_value, "tensor")
    normed = residual_norm(projected, residual_in, norm_gain)
    slot_ids = seq_index * SLOT_DEV + jnp.arange(SLOT_DEV, dtype=jnp.int32)
    source, is_live = slot_source(slot_ids, prompt_lengths, PAGE)
    target = stored_row(source, per_device, seq_count)
    empty_cache = jnp.zeros((SLOT_DEV, kv_width), jnp.bfloat16)
    kv_grid = stacked[:per_device].reshape(per_device, seq_count, 2 * kv_width)
    piece_rows = seq_count * per_device
    found = is_live & (target >= 0) & (target < piece_rows)
    safe_index = jnp.clip(target, 0, piece_rows - 1)
    cache_rows = kv_grid[safe_index % per_device, safe_index // per_device]
    cache_keys = jnp.where(found[:, None], cache_rows[:, :kv_width], empty_cache)
    cache_values = jnp.where(found[:, None], cache_rows[:, kv_width:], empty_cache)
    return (normed, cache_keys, cache_values)


def solution(mesh):
    return jax.shard_map(
        body,
        mesh=mesh,
        in_specs=(
            P("seq", "tensor"),
            P("seq", "tensor"),
            P("seq", "tensor"),
            P("tensor", "seq"),
            P("seq", None),
            P(),
            P(),
        ),
        out_specs=(P("seq", None), P("seq", "tensor"), P("seq", "tensor")),
        check_vma=False,
    )
```
